512 devices in a mesh: seq: 128 (over y, z, core), head: 4 (over x).
Axes of the slice: x: 4, y: 4, z: 16, core: 2. Of those that a mesh axis runs over, the one named last changes fastest.
Arguments:
- tokens: bfloat16 [64, 4, 1024], P('head'), may hold values from -6 to 6
- cache_keys: bfloat16 [64, 4096, 512], P(None, 'seq', 'head'), may hold values from -70 to 70
- cache_values: bfloat16 [64, 4096, 512], P(None, 'seq', 'head'), may hold values from -6 to 6
- held_states: bfloat16 [64, 512, 1024], P(None, 'seq'), may hold values from -6 to 6
- recompute_pos: int32 [64, 512], P(None, 'seq'), may hold values from 0 to 4095, as said below
- cache_len: int32 [64], replicated, may hold values from 1 to 4096
- new_prompt: int32 [64], replicated, may hold values 0 or 1
- w_qkv: bfloat16 [3, 1024, 512], P(None, None, 'head'), may hold values from -0.1875 to 0.1875
- qkv_bias: float32 [3, 512], P(None, 'head'), may hold values from -3 to 3
- w_out: bfloat16 [512, 1024], P('head'), may hold values from -1.5 to 1.5
- out_bias: float32 [1024], replicated, may hold values from -3 to 3
- attn_gain: float32 [1024], replicated, may hold values from 0.1 to 1.9
- attn_shift: float32 [1024], replicated, may hold values from -3 to 3
- w_up: bfloat16 [1024, 2048], P(None, 'head'), may hold values from -0.1875 to 0.1875
- up_bias: float32 [2048], P('head'), may hold values from -3 to 3
- w_down: bfloat16 [2048, 1024], P('head'), may hold values from -0.125 to 0.125
- down_bias: float32 [1024], replicated, may hold values from -3 to 3
- ffn_gain: float32 [1024], replicated, may hold values from 0.1 to 1.9
- ffn_shift: float32 [1024], replicated, may hold values from -3 to 3
Outputs:
- layer_out: bfloat16 [64, 4, 1024], P('head')
The draws below stay inside these ranges and needn't reach their ends.
Inputs may be any that keep to these rules, and one draw needn't show every extreme that they name: `recompute_pos`: columns s * 4 to (s + 1) * 4 - 1 of a row hold distinct positions from s * 32 to (s + 1) * 32 - 1.
All inputs are finite; a program needn't handle non-finite values.
Results may differ from the reference program's by a relative error of at most 0.011.
Values may be sent and summed in bfloat16 or wider, within the bound.
No kernel may reach another device: no remote copies, remote signals or barrier semaphores. Data moves between devices by JAX's collectives and lax.ppermute only.
A program may use at most 192 MiB of HBM per device.

```python
import jax
import jax.numpy as jnp
from jax import lax

D = 1024
HDIM = 64
HEADS = 8
FFW = 2048
STEPS = 4
REQ = 64
CACHE_DEV = 32
AW = 512
RCP_DEV = 4
CACHE = 4096
RC_TOTAL = 512
N_SEQ = 128


def draw_cache_keys(key, part):
    values = jnp.clip(jax.random.normal(key, (REQ, CACHE, AW), jnp.float32), -6.0, 6.0)
    middle = jnp.arange(CACHE) // CACHE_DEV == CACHE // CACHE_DEV // 2
    values = values * jnp.where(middle, 4.0, 1.0)[None, :, None]
    values = jnp.clip(values, -70.0, 70.0)
    return values.astype(jnp.bfloat16)


def draw_cache_len(key, part):
    key_one, key_two, key_three = jax.random.split(key, 3)
    raw_len = jax.random.randint(key_one, (REQ,), 1, CACHE + 1)
    shifts = jax.random.randint(key_two, (REQ,), 0, 4)
    lengths = jnp.maximum(raw_len // jnp.left_shift(jnp.ones((REQ,), jnp.int32), shifts), 1)
    longest = jax.random.randint(key_three, (), 0, REQ)
    return jnp.where(jnp.arange(REQ) == longest, CACHE, lengths).astype(jnp.int32)


def draw_recompute_pos(key, part):
    shards = CACHE // CACHE_DEV
    scores = jax.random.randint(key, (REQ, shards, CACHE_DEV), 0, 1 << 20) * CACHE_DEV + jnp.arange(CACHE_DEV, dtype=jnp.int32)
    ordering = jnp.argsort(scores, axis=-1)
    chosen = ordering[:, :, :RCP_DEV] + (jnp.arange(shards, dtype=jnp.int32) * CACHE_DEV)[None, :, None]
    return chosen.reshape(REQ, shards * RCP_DEV).astype(jnp.int32)


def place_ends(entries, rng, least, high):
    longest = entries.shape.index(max(entries.shape))
    spots = []
    for shift in (0, 1):
        where = [jax.random.randint(jax.random.fold_in(rng, axis), (), 0, length) for axis, length in enumerate(entries.shape)]
        where[longest] = (where[longest] + shift) % entries.shape[longest]
        spots.append(tuple(where))
    return entries.at[spots[0]].set(least).at[spots[1]].set(high)


def block_scale(own_key, shape, pieces, least, high):
    loudness = 1.0
    for position, shards_of in pieces:
        draws = jax.random.uniform(jax.random.fold_in(jax.random.fold_in(own_key, 6), position), (shards_of,), jnp.float32, least / len(pieces), high / len(pieces))
        loudness = loudness * jnp.repeat(jnp.exp(draws), shape[position] // shards_of).reshape((-1,) + (1,) * (len(shape) - 1 - position))
    return loudness


def normal_values(stream_key, shape, deviation, most, cuts=(), kind=jnp.bfloat16):
    drawn = deviation * jax.random.normal(stream_key, shape, jnp.float32)
    if cuts:
        drawn = drawn * block_scale(stream_key, shape, cuts, -0.22, 0.18)
    return jnp.clip(drawn, -most, most).astype(kind)


def setup_inputs(seed: int = 0) -> dict:
    keys = jax.random.split(jax.random.key(seed), 20)
    tokens = normal_values(keys[0], (REQ, STEPS, D), 1.0, 6.0, ((0, 4),))
    cache_keys = draw_cache_keys(jax.random.fold_in(keys[19], 71), 0)
    cache_values = normal_values(keys[2], (REQ, CACHE, AW), 1.0, 6.0, ((1, 128), (2, 4)))
    held_states = normal_values(keys[3], (REQ, RC_TOTAL, D), 1.0, 6.0, ((1, 128),))
    recompute_pos = draw_recompute_pos(jax.random.fold_in(keys[19], 71), 0)
    cache_len = draw_cache_len(jax.random.fold_in(keys[19], 71), 0)
    new_prompt = place_ends((jax.random.randint(keys[6], (REQ,), 0, 8) < 1).astype(jnp.int32), jax.random.fold_in(keys[6], 1), 0, 1)
    w_qkv = normal_values(keys[7], (3, D, AW), D ** -0.5, 0.1875, ((2, 4),))
    qkv_bias = normal_values(keys[8], (3, AW), 0.5, 3.0, ((1, 4),), jnp.float32)
    w_out = normal_values(keys[9], (AW, D), (HDIM // 4) ** -0.5, 1.5, ((0, 4),))
    out_bias = normal_values(keys[10], (D,), 0.5, 3.0, (), jnp.float32)
    attn_gain = jnp.clip(1.0 + 0.18 * jax.random.normal(keys[11], (D,), jnp.float32), 0.1, 1.9)
    attn_shift = normal_values(keys[12], (D,), 0.5, 3.0, (), jnp.float32)
    w_up = normal_values(keys[13], (D, FFW), D ** -0.5, 0.1875, ((1, 4),))
    up_bias = normal_values(keys[14], (FFW,), 0.5, 3.0, ((0, 4),), jnp.float32)
    w_down = normal_values(keys[15], (FFW, D), FFW ** -0.5, 0.125, ((0, 4),))
    down_bias = normal_values(keys[16], (D,), 0.5, 3.0, (), jnp.float32)
    ffn_gain = jnp.clip(1.0 + 0.18 * jax.random.normal(keys[17], (D,), jnp.float32), 0.1, 1.9)
    ffn_shift = normal_values(keys[18], (D,), 0.5, 3.0, (), jnp.float32)
    return {"tokens": tokens, "cache_keys": cache_keys, "cache_values": cache_values, "held_states": held_states, "recompute_pos": recompute_pos, "cache_len": cache_len, "new_prompt": new_prompt, "w_qkv": w_qkv, "qkv_bias": qkv_bias, "w_out": w_out, "out_bias": out_bias, "attn_gain": attn_gain, "attn_shift": attn_shift, "w_up": w_up, "up_bias": up_bias, "w_down": w_down, "down_bias": down_bias, "ffn_gain": ffn_gain, "ffn_shift": ffn_shift}


NEG = -1e+30
EPS = 1e-05

def layer_norm(values, norm_gain, norm_bias):
    center = lax.optimization_barrier(jnp.mean(values, axis=-1, keepdims=True))
    spread = values - center
    second = lax.optimization_barrier(jnp.mean(spread * spread, axis=-1, keepdims=True))
    return spread * lax.rsqrt(second + EPS) * norm_gain.astype(jnp.float32) + norm_bias.astype(jnp.float32)

def merge_pair(first_part, second_part):
    first_max, first_sum, first_out = first_part
    second_max, second_sum, second_out = second_part
    joint_max = jnp.maximum(first_max, second_max)
    first_scale = jnp.exp(first_max - joint_max)
    second_scale = jnp.exp(second_max - joint_max)
    return (joint_max, first_sum * first_scale + second_sum * second_scale, first_out * first_scale[..., None] + second_out * second_scale[..., None])

def partial_attention(queries, keys_here, values_here, visible):
    scores = jnp.einsum('rthe,rphe->rthp', queries.astype(jnp.float32), keys_here.astype(jnp.float32)) * HDIM ** (-0.5)
    highest = lax.optimization_barrier(jnp.max(jnp.where(visible, scores, NEG), axis=-1))
    weights = jnp.exp(jnp.where(visible, scores - highest[..., None], NEG)).astype(jnp.bfloat16)
    totals = lax.optimization_barrier(jnp.sum(weights.astype(jnp.float32), axis=-1))
    blended = jnp.einsum('rthp,rphe->rthe', weights.astype(jnp.float32), values_here.astype(jnp.float32))
    return (highest, totals, blended)

def one_request(inputs):
    queries, new_keys, new_values, keys_all, values_all, length, flagged = inputs
    query_heads = queries.reshape(STEPS, HEADS, HDIM)
    block_queries = jnp.broadcast_to(query_heads[None], (N_SEQ, STEPS, HEADS, HDIM))
    key_blocks = keys_all.reshape(N_SEQ, CACHE_DEV, HEADS, HDIM)
    value_blocks = values_all.reshape(N_SEQ, CACHE_DEV, HEADS, HDIM)
    positions = jnp.arange(CACHE, dtype=jnp.int32).reshape(N_SEQ, CACHE_DEV)
    visible = ((positions < length) & (flagged == 0))[:, None, None, :]
    block_max, block_sum, block_out = partial_attention(block_queries, key_blocks, value_blocks, visible)
    cache_max = lax.optimization_barrier(jnp.max(block_max, axis=0))
    factor = jnp.exp(block_max - cache_max[None])
    cache_sum = lax.optimization_barrier(jnp.sum(block_sum * factor, axis=0))
    cache_out = lax.optimization_barrier(jnp.sum(block_out * factor[..., None], axis=0))
    order_t = jnp.arange(STEPS, dtype=jnp.int32)
    causal = (order_t[:, None] >= order_t[None, :])[None, :, None, :]
    new_max, new_sum, new_out = partial_attention(query_heads[None], new_keys.reshape(1, STEPS, HEADS, HDIM), new_values.reshape(1, STEPS, HEADS, HDIM), causal)
    joint_max, joint_sum, joint_out = merge_pair((cache_max, cache_sum, cache_out), (new_max[0], new_sum[0], new_out[0]))
    return (joint_out / joint_sum[..., None]).reshape(STEPS, AW).astype(jnp.bfloat16)

def reference(tokens, cache_keys, cache_values, held_states, recompute_pos, cache_len, new_prompt, w_qkv, qkv_bias, w_out, out_bias, attn_gain, attn_shift, w_up, up_bias, w_down, down_bias, ffn_gain, ffn_shift):
    flat_tokens = tokens.reshape(REQ * STEPS, D)
    projected = []
    for which in range(3):
        product = jnp.dot(flat_tokens, w_qkv[which], preferred_element_type=jnp.float32) + qkv_bias[which].astype(jnp.float32)
        projected.append(product.astype(jnp.bfloat16).reshape(REQ, STEPS, AW))
    fresh_keys = (jnp.dot(held_states.reshape(REQ * RC_TOTAL, D), w_qkv[1], preferred_element_type=jnp.float32) + qkv_bias[1].astype(jnp.float32)).astype(jnp.bfloat16).reshape(REQ, RC_TOTAL, AW)
    row_index = jnp.arange(REQ, dtype=jnp.int32)[:, None]
    keys_all = cache_keys.at[row_index, recompute_pos.astype(jnp.int32)].set(fresh_keys)
    attended = lax.map(one_request, (projected[0], projected[1], projected[2], keys_all, cache_values, cache_len, new_prompt))
    projection = jnp.dot(attended.reshape(REQ * STEPS, AW), w_out, preferred_element_type=jnp.float32) + out_bias.astype(jnp.float32)
    normed = layer_norm(flat_tokens.astype(jnp.float32) + projection, attn_gain, attn_shift).astype(jnp.bfloat16)
    hidden = jax.nn.gelu(jnp.dot(normed, w_up, preferred_element_type=jnp.float32) + up_bias.astype(jnp.float32), approximate=False).astype(jnp.bfloat16)
    lowered = jnp.dot(hidden, w_down, preferred_element_type=jnp.float32) + down_bias.astype(jnp.float32)
    final = layer_norm(normed.astype(jnp.float32) + lowered, ffn_gain, ffn_shift).astype(jnp.bfloat16)
    return final.reshape(REQ, STEPS, D)
```

```python
import jax
import jax.numpy as jnp
from jax import lax
from jax.sharding import PartitionSpec as P

HDIM = 64


NEG = -1e30
EPS = 1e-05


def layer_norm(values, norm_gain, norm_bias):
    center = jnp.mean(values, axis=-1, keepdims=True)
    spread = values - center
    second = jnp.mean(spread * spread, axis=-1, keepdims=True)
    return spread * lax.rsqrt(second + EPS) * norm_gain + norm_bias


def merge_pair(first_part, second_part):
    first_max, first_sum, first_out = first_part
    second_max, second_sum, second_out = second_part
    joint_max = jnp.maximum(first_max, second_max)
    first_scale = jnp.exp(first_max - joint_max)
    second_scale = jnp.exp(second_max - joint_max)
    return (
        joint_max,
        first_sum * first_scale + second_sum * second_scale,
        first_out * first_scale[..., None] + second_out * second_scale[..., None],
    )


def partial_attention(queries, keys_here, values_here, visible):
    scores = jnp.einsum(
        "rthe,rphe->rthp", queries, keys_here, preferred_element_type=jnp.float32
    ) * HDIM ** (-0.5)
    highest = jnp.max(jnp.where(visible, scores, NEG), axis=-1)
    weights = jnp.exp(jnp.where(visible, scores - highest[..., None], NEG)).astype(jnp.bfloat16)
    totals = jnp.sum(weights.astype(jnp.float32), axis=-1)
    blended = jnp.einsum(
        "rthp,rphe->rthe", weights, values_here, preferred_element_type=jnp.float32
    )
    return (highest, totals, blended)


def seq_merge(block_max, block_sum, block_out):
    n_seq = lax.axis_size("seq")
    head_shape = block_out.shape
    lanes = head_shape[-2] * head_shape[-1]
    rows = block_out.size // lanes
    stat_rows = block_max.size // lanes
    out2 = block_out.reshape(rows, lanes)
    top = block_max.reshape(stat_rows, lanes)
    total = block_sum.reshape(stat_rows, lanes)
    width = head_shape[-1]
    step = 1
    while step < n_seq:
        pairs = [(i, i ^ step) for i in range(n_seq)]
        packed = jnp.concatenate([out2, top, total], axis=0)
        other = lax.ppermute(packed, "seq", pairs)
        o_out = other[:rows]
        o_top = other[rows : rows + stat_rows]
        o_total = other[rows + stat_rows :]
        joint = jnp.maximum(top, o_top)
        mine = jnp.exp(top - joint)
        theirs = jnp.exp(o_top - joint)
        total = total * mine + o_total * theirs
        mine_rows = jnp.repeat(mine.reshape(rows, lanes // width), width, axis=1)
        theirs_rows = jnp.repeat(theirs.reshape(rows, lanes // width), width, axis=1)
        out2 = out2 * mine_rows + o_out * theirs_rows
        top = joint
        step *= 2
    return (
        top.reshape(block_max.shape),
        total.reshape(block_sum.shape),
        out2.reshape(head_shape),
    )


def on_device(
    tokens,
    cache_keys,
    cache_values,
    held_states,
    recompute_pos,
    cache_len,
    new_prompt,
    w_qkv,
    qkv_bias,
    w_out,
    out_bias,
    attn_gain,
    attn_shift,
    w_up,
    up_bias,
    w_down,
    down_bias,
    ffn_gain,
    ffn_shift,
):
    local_width = w_qkv.shape[2]
    local_heads = local_width // HDIM
    requests = cache_keys.shape[0]
    block_len = cache_keys.shape[1]
    own_rows = tokens.shape[0]
    steps_count = tokens.shape[1]
    block_rows = lax.all_gather(tokens, "head", axis=0, tiled=True)
    triple = (
        jnp.einsum("rtd,kdc->rtkc", block_rows, w_qkv, preferred_element_type=jnp.float32)
        + qkv_bias
    )
    triple = triple.astype(jnp.bfloat16).reshape(
        block_rows.shape[0], block_rows.shape[1], 3 * local_width
    )
    gathered = jnp.concatenate([triple, block_rows], axis=2)
    head_shape = (requests, steps_count, local_heads, HDIM)
    queries = gathered[:, :, :local_width].reshape(head_shape)
    new_keys = gathered[:, :, local_width : 2 * local_width].reshape(head_shape)
    new_values = gathered[:, :, 2 * local_width : 3 * local_width].reshape(head_shape)
    fresh_keys = (
        jnp.einsum("rjd,dc->rjc", held_states, w_qkv[1], preferred_element_type=jnp.float32)
        + qkv_bias[1]
    ).astype(jnp.bfloat16)
    offset_pos = lax.axis_index("seq") * block_len
    positions = jnp.arange(block_len, dtype=jnp.int32)
    matches = (recompute_pos - offset_pos)[:, :, None] == positions[None, None, :]
    placed = jnp.einsum(
        "rjp,rjc->rpc", matches.astype(jnp.bfloat16), fresh_keys, preferred_element_type=jnp.float32
    ).astype(jnp.bfloat16)
    replaced = jnp.any(matches, axis=1)
    keys_here = jnp.where(replaced[:, :, None], placed, cache_keys).reshape(
        requests, block_len, local_heads, HDIM
    )
    values_here = cache_values.reshape(requests, block_len, local_heads, HDIM)
    visible = ((offset_pos + positions)[None, :] < cache_len[:, None]) & (new_prompt[:, None] == 0)
    block_max, block_sum, block_out = partial_attention(
        queries, keys_here, values_here, visible[:, None, None, :]
    )
    cache_max, cache_sum, cache_out = seq_merge(block_max, block_sum, block_out)
    order_t = jnp.arange(steps_count, dtype=jnp.int32)
    causal = (order_t[:, None] >= order_t[None, :])[None, :, None, :]
    new_max, new_sum, new_out = partial_attention(queries, new_keys, new_values, causal)
    joint_max, joint_sum, joint_out = merge_pair(
        (cache_max, cache_sum, cache_out), (new_max, new_sum, new_out)
    )
    attended = (
        (joint_out / joint_sum[..., None])
        .astype(jnp.bfloat16)
        .reshape(requests, steps_count, local_width)
    )
    head_terms = jnp.einsum("rtc,cd->rtd", attended, w_out, preferred_element_type=jnp.float32)
    summed = lax.psum(head_terms, "head")
    inputs_all = gathered[:, :, 3 * local_width :]
    normed_all = layer_norm(
        inputs_all.astype(jnp.float32) + summed + out_bias, attn_gain, attn_shift
    ).astype(jnp.bfloat16)
    hidden_all = jax.nn.gelu(
        jnp.einsum("rtd,df->rtf", normed_all, w_up, preferred_element_type=jnp.float32) + up_bias,
        approximate=False,
    ).astype(jnp.bfloat16)
    normed = lax.dynamic_slice_in_dim(normed_all, lax.axis_index("head") * own_rows, own_rows, 0)
    reduced = lax.psum_scatter(
        jnp.einsum("rtf,fd->rtd", hidden_all, w_down, preferred_element_type=jnp.float32),
        "head",
        scatter_dimension=0,
        tiled=True,
    )
    return layer_norm(normed.astype(jnp.float32) + reduced + down_bias, ffn_gain, ffn_shift).astype(
        jnp.bfloat16
    )


def solution(mesh):
    placed = (
        P("head", None, None),
        P(None, "seq", "head"),
        P(None, "seq", "head"),
        P(None, "seq", None),
        P(None, "seq"),
        P(),
        P(),
        P(None, None, "head"),
        P(None, "head"),
        P("head", None),
        P(),
        P(),
        P(),
        P(None, "head"),
        P("head"),
        P("head", None),
        P(),
        P(),
        P(),
    )
    return jax.shard_map(
        on_device, mesh=mesh, in_specs=placed, out_specs=P("head", None, None), check_vma=False
    )
```

```python
import jax
import jax.numpy as jnp
from jax import lax
from jax.sharding import PartitionSpec as P

HDIM = 64


NEG = -1e30
EPS = 1e-05


def layer_norm(values, norm_gain, norm_bias):
    center = jnp.mean(values, axis=-1, keepdims=True)
    spread = values - center
    second = jnp.mean(spread * spread, axis=-1, keepdims=True)
    return spread * lax.rsqrt(second + EPS) * norm_gain + norm_bias


def merge_pair(first_part, second_part):
    first_max, first_sum, first_out = first_part
    second_max, second_sum, second_out = second_part
    joint_max = jnp.maximum(first_max, second_max)
    first_scale = jnp.exp(first_max - joint_max)
    second_scale = jnp.exp(second_max - joint_max)
    return (
        joint_max,
        first_sum * first_scale + second_sum * second_scale,
        first_out * first_scale[..., None] + second_out * second_scale[..., None],
    )


def partial_attention(queries, keys_here, values_here, visible):
    scores = jnp.einsum(
        "rthe,rphe->rthp", queries, keys_here, preferred_element_type=jnp.float32
    ) * HDIM ** (-0.5)
    highest = jnp.max(jnp.where(visible, scores, NEG), axis=-1)
    weights = jnp.exp(jnp.where(visible, scores - highest[..., None], NEG)).astype(jnp.bfloat16)
    totals = jnp.sum(weights.astype(jnp.float32), axis=-1)
    blended = jnp.einsum(
        "rthp,rphe->rthe", weights, values_here, preferred_element_type=jnp.float32
    )
    return (highest, totals, blended)


def seq_merge(block_max, block_sum, block_out):
    n_seq = lax.axis_size("seq")
    head_shape = block_out.shape
    lanes = head_shape[-2] * head_shape[-1]
    rows = block_out.size // lanes
    stat_rows = block_max.size // lanes
    out2 = block_out.reshape(rows, lanes)
    top = block_max.reshape(stat_rows, lanes)
    total = block_sum.reshape(stat_rows, lanes)
    width = head_shape[-1]
    step = 1
    while step < n_seq:
        pairs = [(i, i ^ step) for i in range(n_seq)]
        packed = jnp.concatenate([out2, top, total], axis=0)
        other = lax.ppermute(packed, "seq", pairs)
        o_out = other[:rows]
        o_top = other[rows : rows + stat_rows]
        o_total = other[rows + stat_rows :]
        joint = jnp.maximum(top, o_top)
        mine = jnp.exp(top - joint)
        theirs = jnp.exp(o_top - joint)
        total = total * mine + o_total * theirs
        mine_rows = jnp.repeat(mine.reshape(rows, lanes // width), width, axis=1)
        theirs_rows = jnp.repeat(theirs.reshape(rows, lanes // width), width, axis=1)
        out2 = out2 * mine_rows + o_out * theirs_rows
        top = joint
        step *= 2
    return (
        top.reshape(block_max.shape),
        total.reshape(block_sum.shape),
        out2.reshape(head_shape),
    )


def on_device(
    tokens,
    cache_keys,
    cache_values,
    held_states,
    recompute_pos,
    cache_len,
    new_prompt,
    w_qkv,
    qkv_bias,
    w_out,
    out_bias,
    attn_gain,
    attn_shift,
    w_up,
    up_bias,
    w_down,
    down_bias,
    ffn_gain,
    ffn_shift,
):
    local_width = w_qkv.shape[2]
    local_heads = local_width // HDIM
    requests = cache_keys.shape[0]
    block_len = cache_keys.shape[1]
    own_rows = tokens.shape[0]
    steps_count = tokens.shape[1]
    block_rows = lax.all_gather(tokens, "head", axis=0, tiled=True)
    triple = (
        jnp.einsum("rtd,kdc->rtkc", block_rows, w_qkv, preferred_element_type=jnp.float32)
        + qkv_bias
    )
    triple = triple.astype(jnp.bfloat16).reshape(
        block_rows.shape[0], block_rows.shape[1], 3 * local_width
    )
    gathered = jnp.concatenate([triple, block_rows], axis=2)
    head_shape = (requests, steps_count, local_heads, HDIM)
    queries = gathered[:, :, :local_width].reshape(head_shape)
    new_keys = gathered[:, :, local_width : 2 * local_width].reshape(head_shape)
    new_values = gathered[:, :, 2 * local_width : 3 * local_width].reshape(head_shape)
    fresh_keys = (
        jnp.einsum("rjd,dc->rjc", held_states, w_qkv[1], preferred_element_type=jnp.float32)
        + qkv_bias[1]
    ).astype(jnp.bfloat16)
    offset_pos = lax.axis_index("seq") * block_len
    positions = jnp.arange(block_len, dtype=jnp.int32)
    matches = (recompute_pos - offset_pos)[:, :, None] == positions[None, None, :]
    placed = jnp.einsum(
        "rjp,rjc->rpc", matches.astype(jnp.bfloat16), fresh_keys, preferred_element_type=jnp.float32
    ).astype(jnp.bfloat16)
    replaced = jnp.any(matches, axis=1)
    keys_here = jnp.where(replaced[:, :, None], placed, cache_keys).reshape(
        requests, block_len, local_heads, HDIM
    )
    values_here = cache_values.reshape(requests, block_len, local_heads, HDIM)
    visible = ((offset_pos + positions)[None, :] < cache_len[:, None]) & (new_prompt[:, None] == 0)
    block_max, block_sum, block_out = partial_attention(
        queries, keys_here, values_here, visible[:, None, None, :]
    )
    cache_max, cache_sum, cache_out = seq_merge(block_max, block_sum, block_out)
    order_t = jnp.arange(steps_count, dtype=jnp.int32)
    causal = (order_t[:, None] >= order_t[None, :])[None, :, None, :]
    new_max, new_sum, new_out = partial_attention(queries, new_keys, new_values, causal)
    joint_max, joint_sum, joint_out = merge_pair(
        (cache_max, cache_sum, cache_out), (new_max, new_sum, new_out)
    )
    attended = (
        (joint_out / joint_sum[..., None])
        .astype(jnp.bfloat16)
        .reshape(requests, steps_count, local_width)
    )
    w_out_all = lax.all_gather(w_out, "head", axis=0, tiled=True)
    w_up_all = lax.all_gather(w_up, "head", axis=0)
    up_bias_all = lax.all_gather(up_bias, "head", axis=0)
    w_down_all = lax.all_gather(w_down, "head", axis=0)
    own_attended = lax.all_to_all(attended, "head", 0, 2, tiled=True)
    projected = jnp.einsum(
        "rtc,cd->rtd", own_attended, w_out_all, preferred_element_type=jnp.float32
    )
    normed = layer_norm(
        tokens.astype(jnp.float32) + projected + out_bias, attn_gain, attn_shift
    ).astype(jnp.bfloat16)
    hidden = jax.nn.gelu(
        jnp.einsum("rtd,hdf->rthf", normed, w_up_all, preferred_element_type=jnp.float32)
        + up_bias_all,
        approximate=False,
    ).astype(jnp.bfloat16)
    lowered = jnp.einsum("rthf,hfd->rtd", hidden, w_down_all, preferred_element_type=jnp.float32)
    return layer_norm(normed.astype(jnp.float32) + lowered + down_bias, ffn_gain, ffn_shift).astype(
        jnp.bfloat16
    )

def solution(mesh):
    placed = (
        P("head", None, None),
        P(None, "seq", "head"),
        P(None, "seq", "head"),
        P(None, "seq", None),
        P(None, "seq"),
        P(),
        P(),
        P(None, None, "head"),
        P(None, "head"),
        P("head", None),
        P(),
        P(),
        P(),
        P(None, "head"),
        P("head"),
        P("head", None),
        P(),
        P(),
        P(),
    )
    return jax.shard_map(
        on_device, mesh=mesh, in_specs=placed, out_specs=P("head", None, None), check_vma=False
    )
```

```python
import jax
import jax.numpy as jnp
from jax import lax
from jax.sharding import PartitionSpec as P

HDIM = 64


NEG = -1e30
EPS = 1e-05


def layer_norm(values, norm_gain, norm_bias):
    center = jnp.mean(values, axis=-1, keepdims=True)
    spread = values - center
    second = jnp.mean(spread * spread, axis=-1, keepdims=True)
    return spread * lax.rsqrt(second + EPS) * norm_gain + norm_bias


def merge_pair(first_part, second_part):
    first_max, first_sum, first_out = first_part
    second_max, second_sum, second_out = second_part
    joint_max = jnp.maximum(first_max, second_max)
    first_scale = jnp.exp(first_max - joint_max)
    second_scale = jnp.exp(second_max - joint_max)
    return (
        joint_max,
        first_sum * first_scale + second_sum * second_scale,
        first_out * first_scale[..., None] + second_out * second_scale[..., None],
    )


def partial_attention(queries, keys_here, values_here, visible):
    scores = jnp.einsum(
        "rthe,rphe->rthp", queries, keys_here, preferred_element_type=jnp.float32
    ) * HDIM ** (-0.5)
    highest = jnp.max(jnp.where(visible, scores, NEG), axis=-1)
    weights = jnp.exp(jnp.where(visible, scores - highest[..., None], NEG)).astype(jnp.bfloat16)
    totals = jnp.sum(weights.astype(jnp.float32), axis=-1)
    blended = jnp.einsum(
        "rthp,rphe->rthe", weights, values_here, preferred_element_type=jnp.float32
    )
    return (highest, totals, blended)


def merge_rows(mine, theirs, width):
    top, total, out = mine
    o_top, o_total, o_out = theirs
    joint = jnp.maximum(top, o_top)
    scale = jnp.exp(top - joint)
    o_scale = jnp.exp(o_top - joint)
    out = out * jnp.repeat(scale, width, axis=1) + o_out * jnp.repeat(o_scale, width, axis=1)
    return (joint, total * scale + o_total * o_scale, out)


def exchange(stats, pairs):
    top, total, out = stats
    rows, heads = top.shape
    lanes = out.shape[1]
    flat = jnp.concatenate([top, total], axis=1).reshape(-1)
    fill = (-flat.size) % lanes
    flat = jnp.pad(flat, (0, fill)).reshape(-1, lanes)
    other = lax.ppermute(jnp.concatenate([out, flat], axis=0), "seq", pairs)
    o_out = other[:rows]
    o_flat = other[rows:].reshape(-1)[: rows * 2 * heads].reshape(rows, 2 * heads)
    return (o_flat[:, :heads], o_flat[:, heads:], o_out)


def pick(flag, when_set, when_clear):
    return jax.tree.map(lambda a, b: jnp.where(flag, a, b), when_set, when_clear)


def seq_attend(stats, width):
    n_seq = lax.axis_size("seq")
    me = lax.axis_index("seq")
    rows = stats[2].shape[0]
    bit = 1
    other = exchange(stats, [(i, i ^ bit) for i in range(n_seq)])
    stats = merge_rows(stats, other, width)
    bit *= 2
    scatter_bits = []
    while bit < n_seq and rows % 16 == 0 and len(scatter_bits) < 4:
        half = rows // 2
        upper = (me // bit) % 2 == 1
        low = jax.tree.map(lambda a: a[:half], stats)
        high = jax.tree.map(lambda a: a[half:], stats)
        keep = pick(upper, high, low)
        send = pick(upper, low, high)
        other = exchange(send, [(i, i ^ bit) for i in range(n_seq)])
        stats = merge_rows(keep, other, width)
        scatter_bits.append(bit)
        rows = half
        bit *= 2
    while bit < n_seq:
        other = exchange(stats, [(i, i ^ bit) for i in range(n_seq)])
        stats = merge_rows(stats, other, width)
        bit *= 2
    top, total, out = stats
    attended = (out / jnp.repeat(total, width, axis=1)).astype(jnp.bfloat16)
    for bit in reversed(scatter_bits):
        upper = (me // bit) % 2 == 1
        other = lax.ppermute(attended, "seq", [(i, i ^ bit) for i in range(n_seq)])
        attended = jnp.where(
            upper,
            jnp.concatenate([other, attended], axis=0),
            jnp.concatenate([attended, other], axis=0),
        )
    return attended


def head_gather(x):
    n_head = lax.axis_size("head")
    me = lax.axis_index("head")
    parts = [x]
    for shift in range(1, n_head):
        parts.append(lax.ppermute(x, "head", [(i, (i + shift) % n_head) for i in range(n_head)]))
    stacked = jnp.stack(parts)
    order = (me - jnp.arange(n_head)) % n_head
    return jnp.take(stacked, order, axis=0)

def on_device(
    tokens,
    cache_keys,
    cache_values,
    held_states,
    recompute_pos,
    cache_len,
    new_prompt,
    w_qkv,
    qkv_bias,
    w_out,
    out_bias,
    attn_gain,
    attn_shift,
    w_up,
    up_bias,
    w_down,
    down_bias,
    ffn_gain,
    ffn_shift,
):
    local_width = w_qkv.shape[2]
    local_heads = local_width // HDIM
    requests = cache_keys.shape[0]
    block_len = cache_keys.shape[1]
    own_rows = tokens.shape[0]
    steps_count = tokens.shape[1]
    block_rows = head_gather(tokens).reshape((-1,) + tokens.shape[1:])
    triple = (
        jnp.einsum("rtd,kdc->rtkc", block_rows, w_qkv, preferred_element_type=jnp.float32)
        + qkv_bias
    )
    triple = triple.astype(jnp.bfloat16).reshape(
        block_rows.shape[0], block_rows.shape[1], 3 * local_width
    )
    gathered = jnp.concatenate([triple, block_rows], axis=2)
    head_shape = (requests, steps_count, local_heads, HDIM)
    queries = gathered[:, :, :local_width].reshape(head_shape)
    new_keys = gathered[:, :, local_width : 2 * local_width].reshape(head_shape)
    new_values = gathered[:, :, 2 * local_width : 3 * local_width].reshape(head_shape)
    fresh_keys = (
        jnp.einsum("rjd,dc->rjc", held_states, w_qkv[1], preferred_element_type=jnp.float32)
        + qkv_bias[1]
    ).astype(jnp.bfloat16)
    offset_pos = lax.axis_index("seq") * block_len
    positions = jnp.arange(block_len, dtype=jnp.int32)
    matches = (recompute_pos - offset_pos)[:, :, None] == positions[None, None, :]
    placed = jnp.einsum(
        "rjp,rjc->rpc", matches.astype(jnp.bfloat16), fresh_keys, preferred_element_type=jnp.float32
    ).astype(jnp.bfloat16)
    replaced = jnp.any(matches, axis=1)
    keys_here = jnp.where(replaced[:, :, None], placed, cache_keys).reshape(
        requests, block_len, local_heads, HDIM
    )
    values_here = cache_values.reshape(requests, block_len, local_heads, HDIM)
    visible = ((offset_pos + positions)[None, :] < cache_len[:, None]) & (new_prompt[:, None] == 0)
    block_max, block_sum, block_out = partial_attention(
        queries, keys_here, values_here, visible[:, None, None, :]
    )
    order_t = jnp.arange(steps_count, dtype=jnp.int32)
    causal = (order_t[:, None] >= order_t[None, :])[None, :, None, :]
    new_max, new_sum, new_out = partial_attention(queries, new_keys, new_values, causal)
    rows = requests * steps_count
    flat = lambda m, s, o: (m.reshape(rows, local_heads), s.reshape(rows, local_heads), o.reshape(rows, local_width))
    cache_part = flat(block_max, block_sum, block_out)
    new_part = flat(new_max, new_sum, new_out)
    first = lax.axis_index("seq") == 0
    stats = pick(first, merge_rows(cache_part, new_part, HDIM), cache_part)
    attended = seq_attend(stats, HDIM).reshape(requests, steps_count, local_width)
    w_out_all = lax.all_gather(w_out, "head", axis=0, tiled=True)
    w_up_all = lax.all_gather(w_up, "head", axis=0)
    up_bias_all = head_gather(up_bias)
    w_down_all = lax.all_gather(w_down, "head", axis=0)
    own_attended = lax.all_to_all(attended, "head", 0, 2, tiled=True)
    projected = jnp.einsum(
        "rtc,cd->rtd", own_attended, w_out_all, preferred_element_type=jnp.float32
    )
    normed = layer_norm(
        tokens.astype(jnp.float32) + projected + out_bias, attn_gain, attn_shift
    ).astype(jnp.bfloat16)
    hidden = jax.nn.gelu(
        jnp.einsum("rtd,hdf->rthf", normed, w_up_all, preferred_element_type=jnp.float32)
        + up_bias_all,
        approximate=False,
    ).astype(jnp.bfloat16)
    lowered = jnp.einsum("rthf,hfd->rtd", hidden, w_down_all, preferred_element_type=jnp.float32)
    return layer_norm(normed.astype(jnp.float32) + lowered + down_bias, ffn_gain, ffn_shift).astype(
        jnp.bfloat16
    )

def solution(mesh):
    placed = (
        P("head", None, None),
        P(None, "seq", "head"),
        P(None, "seq", "head"),
        P(None, "seq", None),
        P(None, "seq"),
        P(),
        P(),
        P(None, None, "head"),
        P(None, "head"),
        P("head", None),
        P(),
        P(),
        P(),
        P(None, "head"),
        P("head"),
        P("head", None),
        P(),
        P(),
        P(),
    )
    return jax.shard_map(
        on_device, mesh=mesh, in_specs=placed, out_specs=P("head", None, None), check_vma=False
    )
```

```python
import jax
import jax.numpy as jnp
from jax import lax
from jax.sharding import PartitionSpec as P

HDIM = 64


NEG = -1e30
EPS = 1e-05


def layer_norm(values, norm_gain, norm_bias):
    center = jnp.mean(values, axis=-1, keepdims=True)
    spread = values - center
    second = jnp.mean(spread * spread, axis=-1, keepdims=True)
    return spread * lax.rsqrt(second + EPS) * norm_gain + norm_bias


def merge_pair(first_part, second_part):
    first_max, first_sum, first_out = first_part
    second_max, second_sum, second_out = second_part
    joint_max = jnp.maximum(first_max, second_max)
    first_scale = jnp.exp(first_max - joint_max)
    second_scale = jnp.exp(second_max - joint_max)
    return (
        joint_max,
        first_sum * first_scale + second_sum * second_scale,
        first_out * first_scale[..., None] + second_out * second_scale[..., None],
    )


def partial_attention(queries, keys_here, values_here, visible):
    scores = jnp.einsum(
        "rthe,rphe->rthp", queries, keys_here, preferred_element_type=jnp.float32
    ) * HDIM ** (-0.5)
    highest = jnp.max(jnp.where(visible, scores, NEG), axis=-1)
    weights = jnp.exp(jnp.where(visible, scores - highest[..., None], NEG)).astype(jnp.bfloat16)
    totals = jnp.sum(weights.astype(jnp.float32), axis=-1)
    blended = jnp.einsum(
        "rthp,rphe->rthe", weights, values_here, preferred_element_type=jnp.float32
    )
    return (highest, totals, blended)


def merge_rows(mine, theirs, width):
    top, total, out = mine
    o_top, o_total, o_out = theirs
    joint = jnp.maximum(top, o_top)
    scale = jnp.exp(top - joint)
    o_scale = jnp.exp(o_top - joint)
    out = out * jnp.repeat(scale, width, axis=1) + o_out * jnp.repeat(o_scale, width, axis=1)
    return (joint, total * scale + o_total * o_scale, out)


def exchange(stats, pairs):
    top, total, out = stats
    rows, heads = top.shape
    lanes = out.shape[1]
    flat = jnp.concatenate([top, total], axis=1).reshape(-1)
    fill = (-flat.size) % lanes
    flat = jnp.pad(flat, (0, fill)).reshape(-1, lanes)
    other = lax.ppermute(jnp.concatenate([out, flat], axis=0), "seq", pairs)
    o_out = other[:rows]
    o_flat = other[rows:].reshape(-1)[: rows * 2 * heads].reshape(rows, 2 * heads)
    return (o_flat[:, :heads], o_flat[:, heads:], o_out)


def pick(flag, when_set, when_clear):
    return jax.tree.map(lambda a, b: jnp.where(flag, a, b), when_set, when_clear)


def seq_attend(stats, width):
    n_seq = lax.axis_size("seq")
    me = lax.axis_index("seq")
    rows = stats[2].shape[0]
    bit = 1
    scatter_bits = []
    while bit < n_seq and rows % 16 == 0 and len(scatter_bits) < 2:
        half = rows // 2
        upper = (me // bit) % 2 == 1
        low = jax.tree.map(lambda a: a[:half], stats)
        high = jax.tree.map(lambda a: a[half:], stats)
        keep = pick(upper, high, low)
        send = pick(upper, low, high)
        other = exchange(send, [(i, i ^ bit) for i in range(n_seq)])
        stats = merge_rows(keep, other, width)
        scatter_bits.append(bit)
        rows = half
        bit *= 2
    while bit < n_seq:
        other = exchange(stats, [(i, i ^ bit) for i in range(n_seq)])
        stats = merge_rows(stats, other, width)
        bit *= 2
    top, total, out = stats
    attended = (out / jnp.repeat(total, width, axis=1)).astype(jnp.bfloat16)
    for bit in reversed(scatter_bits):
        upper = (me // bit) % 2 == 1
        other = lax.ppermute(attended, "seq", [(i, i ^ bit) for i in range(n_seq)])
        attended = jnp.where(
            upper,
            jnp.concatenate([other, attended], axis=0),
            jnp.concatenate([attended, other], axis=0),
        )
    return attended


def head_gather(x):
    n_head = lax.axis_size("head")
    me = lax.axis_index("head")
    parts = [x]
    for shift in range(1, n_head):
        parts.append(lax.ppermute(x, "head", [(i, (i + shift) % n_head) for i in range(n_head)]))
    stacked = jnp.stack(parts)
    order = (me - jnp.arange(n_head)) % n_head
    return jnp.take(stacked, order, axis=0)

def on_device(
    tokens,
    cache_keys,
    cache_values,
    held_states,
    recompute_pos,
    cache_len,
    new_prompt,
    w_qkv,
    qkv_bias,
    w_out,
    out_bias,
    attn_gain,
    attn_shift,
    w_up,
    up_bias,
    w_down,
    down_bias,
    ffn_gain,
    ffn_shift,
):
    local_width = w_qkv.shape[2]
    local_heads = local_width // HDIM
    requests = cache_keys.shape[0]
    block_len = cache_keys.shape[1]
    own_rows = tokens.shape[0]
    steps_count = tokens.shape[1]
    block_rows = head_gather(tokens).reshape((-1,) + tokens.shape[1:])
    triple = (
        jnp.einsum("rtd,kdc->rtkc", block_rows, w_qkv, preferred_element_type=jnp.float32)
        + qkv_bias
    )
    triple = triple.astype(jnp.bfloat16).reshape(
        block_rows.shape[0], block_rows.shape[1], 3 * local_width
    )
    gathered = jnp.concatenate([triple, block_rows], axis=2)
    head_shape = (requests, steps_count, local_heads, HDIM)
    queries = gathered[:, :, :local_width].reshape(head_shape)
    new_keys = gathered[:, :, local_width : 2 * local_width].reshape(head_shape)
    new_values = gathered[:, :, 2 * local_width : 3 * local_width].reshape(head_shape)
    fresh_keys = (
        jnp.einsum("rjd,dc->rjc", held_states, w_qkv[1], preferred_element_type=jnp.float32)
        + qkv_bias[1]
    ).astype(jnp.bfloat16)
    offset_pos = lax.axis_index("seq") * block_len
    positions = jnp.arange(block_len, dtype=jnp.int32)
    matches = (recompute_pos - offset_pos)[:, :, None] == positions[None, None, :]
    placed = jnp.einsum(
        "rjp,rjc->rpc", matches.astype(jnp.bfloat16), fresh_keys, preferred_element_type=jnp.float32
    ).astype(jnp.bfloat16)
    replaced = jnp.any(matches, axis=1)
    keys_here = jnp.where(replaced[:, :, None], placed, cache_keys).reshape(
        requests, block_len, local_heads, HDIM
    )
    values_here = cache_values.reshape(requests, block_len, local_heads, HDIM)
    visible = ((offset_pos + positions)[None, :] < cache_len[:, None]) & (new_prompt[:, None] == 0)
    block_max, block_sum, block_out = partial_attention(
        queries, keys_here, values_here, visible[:, None, None, :]
    )
    order_t = jnp.arange(steps_count, dtype=jnp.int32)
    causal = (order_t[:, None] >= order_t[None, :])[None, :, None, :]
    new_max, new_sum, new_out = partial_attention(queries, new_keys, new_values, causal)
    rows = requests * steps_count
    flat = lambda m, s, o: (m.reshape(rows, local_heads), s.reshape(rows, local_heads), o.reshape(rows, local_width))
    cache_part = flat(block_max, block_sum, block_out)
    new_part = flat(new_max, new_sum, new_out)
    first = lax.axis_index("seq") == 0
    stats = pick(first, merge_rows(cache_part, new_part, HDIM), cache_part)
    attended = seq_attend(stats, HDIM).reshape(requests, steps_count, local_width)
    w_out_all = lax.all_gather(w_out, "head", axis=0, tiled=True)
    core = lax.axis_index("seq") % 2
    ffw_half = w_up.shape[1] // 2
    w_up_all = lax.all_gather(
        lax.dynamic_slice_in_dim(w_up, core * ffw_half, ffw_half, 1), "head", axis=0
    )
    up_bias_all = head_gather(lax.dynamic_slice_in_dim(up_bias, core * ffw_half, ffw_half, 0))
    w_down_all = lax.all_gather(
        lax.dynamic_slice_in_dim(w_down, core * ffw_half, ffw_half, 0), "head", axis=0
    )
    own_attended = lax.all_to_all(attended, "head", 0, 2, tiled=True)
    projected = jnp.einsum(
        "rtc,cd->rtd", own_attended, w_out_all, preferred_element_type=jnp.float32
    )
    normed = layer_norm(
        tokens.astype(jnp.float32) + projected + out_bias, attn_gain, attn_shift
    ).astype(jnp.bfloat16)
    hidden = jax.nn.gelu(
        jnp.einsum("rtd,hdf->rthf", normed, w_up_all, preferred_element_type=jnp.float32)
        + up_bias_all,
        approximate=False,
    ).astype(jnp.bfloat16)
    lowered = jnp.einsum("rthf,hfd->rtd", hidden, w_down_all, preferred_element_type=jnp.float32)
    n_seq = lax.axis_size("seq")
    lowered = lowered + lax.ppermute(lowered, "seq", [(i, i ^ 1) for i in range(n_seq)])
    return layer_norm(normed.astype(jnp.float32) + lowered + down_bias, ffn_gain, ffn_shift).astype(
        jnp.bfloat16
    )

def solution(mesh):
    placed = (
        P("head", None, None),
        P(None, "seq", "head"),
        P(None, "seq", "head"),
        P(None, "seq", None),
        P(None, "seq"),
        P(),
        P(),
        P(None, None, "head"),
        P(None, "head"),
        P("head", None),
        P(),
        P(),
        P(),
        P(None, "head"),
        P("head"),
        P("head", None),
        P(),
        P(),
        P(),
    )
    return jax.shard_map(
        on_device, mesh=mesh, in_specs=placed, out_specs=P("head", None, None), check_vma=False
    )
```

```python
import jax
import jax.numpy as jnp
from jax import lax
from jax.sharding import PartitionSpec as P

HDIM = 64


NEG = -1e30
EPS = 1e-05


def layer_norm(values, norm_gain, norm_bias):
    center = jnp.mean(values, axis=-1, keepdims=True)
    spread = values - center
    second = jnp.mean(spread * spread, axis=-1, keepdims=True)
    return spread * lax.rsqrt(second + EPS) * norm_gain + norm_bias


def merge_pair(first_part, second_part):
    first_max, first_sum, first_out = first_part
    second_max, second_sum, second_out = second_part
    joint_max = jnp.maximum(first_max, second_max)
    first_scale = jnp.exp(first_max - joint_max)
    second_scale = jnp.exp(second_max - joint_max)
    return (
        joint_max,
        first_sum * first_scale + second_sum * second_scale,
        first_out * first_scale[..., None] + second_out * second_scale[..., None],
    )


def partial_attention(queries, keys_here, values_here, visible):
    scores = jnp.einsum(
        "rthe,rphe->rthp", queries, keys_here, preferred_element_type=jnp.float32
    ) * HDIM ** (-0.5)
    highest = jnp.max(jnp.where(visible, scores, NEG), axis=-1)
    weights = jnp.exp(jnp.where(visible, scores - highest[..., None], NEG)).astype(jnp.bfloat16)
    totals = jnp.sum(weights.astype(jnp.float32), axis=-1)
    blended = jnp.einsum(
        "rthp,rphe->rthe", weights, values_here, preferred_element_type=jnp.float32
    )
    return (highest, totals, blended)


def merge_rows(mine, theirs, width):
    top, total, out = mine
    o_top, o_total, o_out = theirs
    joint = jnp.maximum(top, o_top)
    scale = jnp.exp(top - joint)
    o_scale = jnp.exp(o_top - joint)
    out = out * jnp.repeat(scale, width, axis=1) + o_out * jnp.repeat(o_scale, width, axis=1)
    return (joint, total * scale + o_total * o_scale, out)


def exchange(stats, pairs):
    top, total, out = stats
    rows, heads = top.shape
    lanes = out.shape[1]
    flat = jnp.concatenate([top, total], axis=1).reshape(-1)
    fill = (-flat.size) % lanes
    flat = jnp.pad(flat, (0, fill)).reshape(-1, lanes)
    other = lax.ppermute(jnp.concatenate([out, flat], axis=0), "seq", pairs)
    o_out = other[:rows]
    o_flat = other[rows:].reshape(-1)[: rows * 2 * heads].reshape(rows, 2 * heads)
    return (o_flat[:, :heads], o_flat[:, heads:], o_out)


def pick(flag, when_set, when_clear):
    return jax.tree.map(lambda a, b: jnp.where(flag, a, b), when_set, when_clear)


def seq_attend(stats, width):
    n_seq = lax.axis_size("seq")
    me = lax.axis_index("seq")
    rows = stats[2].shape[0]
    bit = 1
    scatter_bits = []
    while bit < n_seq and rows % 16 == 0 and len(scatter_bits) < 2:
        half = rows // 2
        upper = (me // bit) % 2 == 1
        low = jax.tree.map(lambda a: a[:half], stats)
        high = jax.tree.map(lambda a: a[half:], stats)
        keep = pick(upper, high, low)
        send = pick(upper, low, high)
        other = exchange(send, [(i, i ^ bit) for i in range(n_seq)])
        stats = merge_rows(keep, other, width)
        scatter_bits.append(bit)
        rows = half
        bit *= 2
    while bit < n_seq:
        other = exchange(stats, [(i, i ^ bit) for i in range(n_seq)])
        stats = merge_rows(stats, other, width)
        bit *= 2
    top, total, out = stats
    attended = (out / jnp.repeat(total, width, axis=1)).astype(jnp.bfloat16)
    for bit in reversed(scatter_bits):
        upper = (me // bit) % 2 == 1
        other = lax.ppermute(attended, "seq", [(i, i ^ bit) for i in range(n_seq)])
        attended = jnp.where(
            upper,
            jnp.concatenate([other, attended], axis=0),
            jnp.concatenate([attended, other], axis=0),
        )
    return attended


def head_gather(x):
    n_head = lax.axis_size("head")
    me = lax.axis_index("head")
    parts = [x]
    for shift in range(1, n_head):
        parts.append(lax.ppermute(x, "head", [(i, (i + shift) % n_head) for i in range(n_head)]))
    stacked = jnp.stack(parts)
    order = (me - jnp.arange(n_head)) % n_head
    return jnp.take(stacked, order, axis=0)

def on_device(
    tokens,
    cache_keys,
    cache_values,
    held_states,
    recompute_pos,
    cache_len,
    new_prompt,
    w_qkv,
    qkv_bias,
    w_out,
    out_bias,
    attn_gain,
    attn_shift,
    w_up,
    up_bias,
    w_down,
    down_bias,
    ffn_gain,
    ffn_shift,
):
    local_width = w_qkv.shape[2]
    local_heads = local_width // HDIM
    requests = cache_keys.shape[0]
    block_len = cache_keys.shape[1]
    own_rows = tokens.shape[0]
    steps_count = tokens.shape[1]
    block_rows = head_gather(tokens).reshape((-1,) + tokens.shape[1:])
    triple = (
        jnp.einsum("rtd,kdc->rtkc", block_rows, w_qkv, preferred_element_type=jnp.float32)
        + qkv_bias
    )
    triple = triple.astype(jnp.bfloat16).reshape(
        block_rows.shape[0], block_rows.shape[1], 3 * local_width
    )
    gathered = jnp.concatenate([triple, block_rows], axis=2)
    head_shape = (requests, steps_count, local_heads, HDIM)
    queries = gathered[:, :, :local_width].reshape(head_shape)
    new_keys = gathered[:, :, local_width : 2 * local_width].reshape(head_shape)
    new_values = gathered[:, :, 2 * local_width : 3 * local_width].reshape(head_shape)
    fresh_keys = (
        jnp.einsum("rjd,dc->rjc", held_states, w_qkv[1], preferred_element_type=jnp.float32)
        + qkv_bias[1]
    ).astype(jnp.bfloat16)
    offset_pos = lax.axis_index("seq") * block_len
    positions = jnp.arange(block_len, dtype=jnp.int32)
    matches = (recompute_pos - offset_pos)[:, :, None] == positions[None, None, :]
    placed = jnp.einsum(
        "rjp,rjc->rpc", matches.astype(jnp.bfloat16), fresh_keys, preferred_element_type=jnp.float32
    ).astype(jnp.bfloat16)
    replaced = jnp.any(matches, axis=1)
    keys_here = jnp.where(replaced[:, :, None], placed, cache_keys).reshape(
        requests, block_len, local_heads, HDIM
    )
    values_here = cache_values.reshape(requests, block_len, local_heads, HDIM)
    visible = ((offset_pos + positions)[None, :] < cache_len[:, None]) & (new_prompt[:, None] == 0)
    block_max, block_sum, block_out = partial_attention(
        queries, keys_here, values_here, visible[:, None, None, :]
    )
    order_t = jnp.arange(steps_count, dtype=jnp.int32)
    causal = (order_t[:, None] >= order_t[None, :])[None, :, None, :]
    new_max, new_sum, new_out = partial_attention(queries, new_keys, new_values, causal)
    rows = requests * steps_count
    flat = lambda m, s, o: (m.reshape(rows, local_heads), s.reshape(rows, local_heads), o.reshape(rows, local_width))
    cache_part = flat(block_max, block_sum, block_out)
    new_part = flat(new_max, new_sum, new_out)
    first = lax.axis_index("seq") == 0
    stats = pick(first, merge_rows(cache_part, new_part, HDIM), cache_part)
    attended = seq_attend(stats, HDIM).reshape(requests, steps_count, local_width)
    n_seq = lax.axis_size("seq")
    core = lax.axis_index("seq") % 2
    pair = [(i, i ^ 1) for i in range(n_seq)]
    d_half = w_out.shape[1] // 2
    w_out_all = lax.all_gather(
        lax.dynamic_slice_in_dim(w_out, core * d_half, d_half, 1), "head", axis=0, tiled=True
    )
    ffw_half = w_up.shape[1] // 2
    bias_half = lax.dynamic_slice_in_dim(up_bias, core * ffw_half, ffw_half, 0)
    bias_hi = lax.reduce_precision(bias_half, exponent_bits=8, mantissa_bits=7)
    rest = bias_half - bias_hi
    bias_mid = lax.reduce_precision(rest, exponent_bits=8, mantissa_bits=7)
    bias_lo = rest - bias_mid
    pieces = jnp.stack([bias_hi, bias_mid, bias_lo]).astype(jnp.bfloat16)
    pieces = jnp.pad(pieces, ((0, 5), (0, 0)))
    up_rows = w_up.shape[0]
    w_up_all = lax.all_gather(
        jnp.concatenate(
            [lax.dynamic_slice_in_dim(w_up, core * ffw_half, ffw_half, 1), pieces], axis=0
        ),
        "head",
        axis=0,
    )
    got = w_up_all[:, up_rows : up_rows + 3].astype(jnp.float32)
    up_bias_all = got[:, 0] + got[:, 1] + got[:, 2]
    w_up_all = w_up_all[:, :up_rows]
    w_down_all = lax.all_gather(
        lax.dynamic_slice_in_dim(w_down, core * ffw_half, ffw_half, 0), "head", axis=0
    )
    own_attended = lax.all_to_all(attended, "head", 0, 2, tiled=True)
    projected = jnp.einsum(
        "rtc,cd->rtd", own_attended, w_out_all, preferred_element_type=jnp.float32
    )
    other_half = lax.ppermute(projected, "seq", pair)
    projected = jnp.where(
        core == 1,
        jnp.concatenate([other_half, projected], axis=2),
        jnp.concatenate([projected, other_half], axis=2),
    )
    normed = layer_norm(
        tokens.astype(jnp.float32) + projected + out_bias, attn_gain, attn_shift
    ).astype(jnp.bfloat16)
    hidden = jax.nn.gelu(
        jnp.einsum("rtd,hdf->rthf", normed, w_up_all, preferred_element_type=jnp.float32)
        + up_bias_all,
        approximate=False,
    ).astype(jnp.bfloat16)
    lowered = jnp.einsum("rthf,hfd->rtd", hidden, w_down_all, preferred_element_type=jnp.float32)
    lowered = lowered + lax.ppermute(lowered, "seq", pair)
    return layer_norm(normed.astype(jnp.float32) + lowered + down_bias, ffn_gain, ffn_shift).astype(
        jnp.bfloat16
    )

def solution(mesh):
    placed = (
        P("head", None, None),
        P(None, "seq", "head"),
        P(None, "seq", "head"),
        P(None, "seq", None),
        P(None, "seq"),
        P(),
        P(),
        P(None, None, "head"),
        P(None, "head"),
        P("head", None),
        P(),
        P(),
        P(),
        P(None, "head"),
        P("head"),
        P("head", None),
        P(),
        P(),
        P(),
    )
    return jax.shard_map(
        on_device, mesh=mesh, in_specs=placed, out_specs=P("head", None, None), check_vma=False
    )
```

```python
import jax
import jax.numpy as jnp
from jax import lax
from jax.sharding import PartitionSpec as P

HDIM = 64


NEG = -1e30
EPS = 1e-05


def layer_norm(values, norm_gain, norm_bias):
    center = jnp.mean(values, axis=-1, keepdims=True)
    spread = values - center
    second = jnp.mean(spread * spread, axis=-1, keepdims=True)
    return spread * lax.rsqrt(second + EPS) * norm_gain + norm_bias


def merge_pair(first_part, second_part):
    first_max, first_sum, first_out = first_part
    second_max, second_sum, second_out = second_part
    joint_max = jnp.maximum(first_max, second_max)
    first_scale = jnp.exp(first_max - joint_max)
    second_scale = jnp.exp(second_max - joint_max)
    return (
        joint_max,
        first_sum * first_scale + second_sum * second_scale,
        first_out * first_scale[..., None] + second_out * second_scale[..., None],
    )


def partial_attention(queries, keys_here, values_here, visible):
    scores = jnp.einsum(
        "rthe,rphe->rthp", queries, keys_here, preferred_element_type=jnp.float32
    ) * HDIM ** (-0.5)
    highest = jnp.max(jnp.where(visible, scores, NEG), axis=-1)
    weights = jnp.exp(jnp.where(visible, scores - highest[..., None], NEG)).astype(jnp.bfloat16)
    totals = jnp.sum(weights.astype(jnp.float32), axis=-1)
    blended = jnp.einsum(
        "rthp,rphe->rthe", weights, values_here, preferred_element_type=jnp.float32
    )
    return (highest, totals, blended)


def merge_rows(mine, theirs, width):
    top, total, out = mine
    o_top, o_total, o_out = theirs
    joint = jnp.maximum(top, o_top)
    scale = jnp.exp(top - joint)
    o_scale = jnp.exp(o_top - joint)
    out = out * jnp.repeat(scale, width, axis=1) + o_out * jnp.repeat(o_scale, width, axis=1)
    return (joint, total * scale + o_total * o_scale, out)


def exchange(stats, pairs):
    top, total, out = stats
    rows, heads = top.shape
    lanes = out.shape[1]
    flat = jnp.concatenate([top, total], axis=1).reshape(-1)
    fill = (-flat.size) % lanes
    flat = jnp.pad(flat, (0, fill)).reshape(-1, lanes)
    other = lax.ppermute(jnp.concatenate([out, flat], axis=0), "seq", pairs)
    o_out = other[:rows]
    o_flat = other[rows:].reshape(-1)[: rows * 2 * heads].reshape(rows, 2 * heads)
    return (o_flat[:, :heads], o_flat[:, heads:], o_out)


def pick(flag, when_set, when_clear):
    return jax.tree.map(lambda a, b: jnp.where(flag, a, b), when_set, when_clear)


def seq_attend(stats, width):
    n_seq = lax.axis_size("seq")
    me = lax.axis_index("seq")
    rows = stats[2].shape[0]
    bit = 1
    scatter_bits = []
    while bit < n_seq and rows % 16 == 0 and len(scatter_bits) < 2:
        half = rows // 2
        upper = (me // bit) % 2 == 1
        low = jax.tree.map(lambda a: a[:half], stats)
        high = jax.tree.map(lambda a: a[half:], stats)
        keep = pick(upper, high, low)
        send = pick(upper, low, high)
        other = exchange(send, [(i, i ^ bit) for i in range(n_seq)])
        stats = merge_rows(keep, other, width)
        scatter_bits.append(bit)
        rows = half
        bit *= 2
    while bit < n_seq:
        other = exchange(stats, [(i, i ^ bit) for i in range(n_seq)])
        stats = merge_rows(stats, other, width)
        bit *= 2
    top, total, out = stats
    attended = (out / jnp.repeat(total, width, axis=1)).astype(jnp.bfloat16)
    for bit in reversed(scatter_bits):
        upper = (me // bit) % 2 == 1
        other = lax.ppermute(attended, "seq", [(i, i ^ bit) for i in range(n_seq)])
        attended = jnp.where(
            upper,
            jnp.concatenate([other, attended], axis=0),
            jnp.concatenate([attended, other], axis=0),
        )
    return attended


def head_gather(x):
    n_head = lax.axis_size("head")
    me = lax.axis_index("head")
    parts = [x]
    for shift in range(1, n_head):
        parts.append(lax.ppermute(x, "head", [(i, (i + shift) % n_head) for i in range(n_head)]))
    stacked = jnp.stack(parts)
    order = (me - jnp.arange(n_head)) % n_head
    return jnp.take(stacked, order, axis=0)

def on_device(
    tokens,
    cache_keys,
    cache_values,
    held_states,
    recompute_pos,
    cache_len,
    new_prompt,
    w_qkv,
    qkv_bias,
    w_out,
    out_bias,
    attn_gain,
    attn_shift,
    w_up,
    up_bias,
    w_down,
    down_bias,
    ffn_gain,
    ffn_shift,
):
    local_width = w_qkv.shape[2]
    local_heads = local_width // HDIM
    requests = cache_keys.shape[0]
    block_len = cache_keys.shape[1]
    own_rows = tokens.shape[0]
    steps_count = tokens.shape[1]
    block_rows = head_gather(tokens).reshape((-1,) + tokens.shape[1:])
    triple = (
        jnp.einsum("rtd,kdc->rtkc", block_rows, w_qkv, preferred_element_type=jnp.float32)
        + qkv_bias
    )
    triple = triple.astype(jnp.bfloat16).reshape(
        block_rows.shape[0], block_rows.shape[1], 3 * local_width
    )
    gathered = jnp.concatenate([triple, block_rows], axis=2)
    head_shape = (requests, steps_count, local_heads, HDIM)
    queries = gathered[:, :, :local_width].reshape(head_shape)
    new_keys = gathered[:, :, local_width : 2 * local_width].reshape(head_shape)
    new_values = gathered[:, :, 2 * local_width : 3 * local_width].reshape(head_shape)
    fresh_keys = (
        jnp.einsum("rjd,dc->rjc", held_states, w_qkv[1], preferred_element_type=jnp.float32)
        + qkv_bias[1]
    ).astype(jnp.bfloat16)
    offset_pos = lax.axis_index("seq") * block_len
    positions = jnp.arange(block_len, dtype=jnp.int32)
    matches = (recompute_pos - offset_pos)[:, :, None] == positions[None, None, :]
    placed = jnp.einsum(
        "rjp,rjc->rpc", matches.astype(jnp.bfloat16), fresh_keys, preferred_element_type=jnp.float32
    ).astype(jnp.bfloat16)
    replaced = jnp.any(matches, axis=1)
    keys_here = jnp.where(replaced[:, :, None], placed, cache_keys).reshape(
        requests, block_len, local_heads, HDIM
    )
    values_here = cache_values.reshape(requests, block_len, local_heads, HDIM)
    visible = ((offset_pos + positions)[None, :] < cache_len[:, None]) & (new_prompt[:, None] == 0)
    block_max, block_sum, block_out = partial_attention(
        queries, keys_here, values_here, visible[:, None, None, :]
    )
    order_t = jnp.arange(steps_count, dtype=jnp.int32)
    causal = (order_t[:, None] >= order_t[None, :])[None, :, None, :]
    new_max, new_sum, new_out = partial_attention(queries, new_keys, new_values, causal)
    rows = requests * steps_count
    flat = lambda m, s, o: (m.reshape(rows, local_heads), s.reshape(rows, local_heads), o.reshape(rows, local_width))
    cache_part = flat(block_max, block_sum, block_out)
    new_part = flat(new_max, new_sum, new_out)
    first = lax.axis_index("seq") == 0
    stats = pick(first, merge_rows(cache_part, new_part, HDIM), cache_part)
    attended = seq_attend(stats, HDIM).reshape(requests, steps_count, local_width)
    n_seq = lax.axis_size("seq")
    core = lax.axis_index("seq") % 2
    pair = [(i, i ^ 1) for i in range(n_seq)]
    d_half = w_out.shape[1] // 2
    w_out_half = lax.dynamic_slice_in_dim(w_out, core * d_half, d_half, 1)
    ffw_half = w_up.shape[1] // 2
    bias_half = lax.dynamic_slice_in_dim(up_bias, core * ffw_half, ffw_half, 0)
    bias_hi = lax.reduce_precision(bias_half, exponent_bits=8, mantissa_bits=7)
    rest = bias_half - bias_hi
    bias_mid = lax.reduce_precision(rest, exponent_bits=8, mantissa_bits=7)
    bias_lo = rest - bias_mid
    pieces = jnp.stack([bias_hi, bias_mid, bias_lo]).astype(jnp.bfloat16)
    pieces = jnp.pad(pieces, ((0, 5), (0, 0)))
    up_rows = w_up.shape[0]
    out_rows = w_out_half.size // ffw_half
    w_up_all = lax.all_gather(
        jnp.concatenate(
            [
                lax.dynamic_slice_in_dim(w_up, core * ffw_half, ffw_half, 1),
                pieces,
                w_out_half.reshape(out_rows, ffw_half),
            ],
            axis=0,
        ),
        "head",
        axis=0,
    )
    got = w_up_all[:, up_rows : up_rows + 3].astype(jnp.float32)
    up_bias_all = got[:, 0] + got[:, 1] + got[:, 2]
    w_out_all = w_up_all[:, up_rows + 8 :].reshape(-1, d_half)
    w_up_all = w_up_all[:, :up_rows]
    w_down_all = lax.all_gather(
        lax.dynamic_slice_in_dim(w_down, core * ffw_half, ffw_half, 0), "head", axis=0
    )
    own_attended = lax.all_to_all(attended, "head", 0, 2, tiled=True)
    projected = jnp.einsum(
        "rtc,cd->rtd", own_attended, w_out_all, preferred_element_type=jnp.float32
    )
    other_half = lax.ppermute(projected, "seq", pair)
    projected = jnp.where(
        core == 1,
        jnp.concatenate([other_half, projected], axis=2),
        jnp.concatenate([projected, other_half], axis=2),
    )
    normed = layer_norm(
        tokens.astype(jnp.float32) + projected + out_bias, attn_gain, attn_shift
    ).astype(jnp.bfloat16)
    hidden = jax.nn.gelu(
        jnp.einsum("rtd,hdf->rthf", normed, w_up_all, preferred_element_type=jnp.float32)
        + up_bias_all,
        approximate=False,
    ).astype(jnp.bfloat16)
    lowered = jnp.einsum("rthf,hfd->rtd", hidden, w_down_all, preferred_element_type=jnp.float32)
    lowered = lowered + lax.ppermute(lowered, "seq", pair)
    return layer_norm(normed.astype(jnp.float32) + lowered + down_bias, ffn_gain, ffn_shift).astype(
        jnp.bfloat16
    )


def solution(mesh):
    placed = (
        P("head", None, None),
        P(None, "seq", "head"),
        P(None, "seq", "head"),
        P(None, "seq", None),
        P(None, "seq"),
        P(),
        P(),
        P(None, None, "head"),
        P(None, "head"),
        P("head", None),
        P(),
        P(),
        P(),
        P(None, "head"),
        P("head"),
        P("head", None),
        P(),
        P(),
        P(),
    )
    return jax.shard_map(
        on_device, mesh=mesh, in_specs=placed, out_specs=P("head", None, None), check_vma=False
    )
```

```python
import jax
import jax.numpy as jnp
from jax import lax
from jax.sharding import PartitionSpec as P

HDIM = 64


NEG = -1e30
EPS = 1e-05


def layer_norm(values, norm_gain, norm_bias):
    center = jnp.mean(values, axis=-1, keepdims=True)
    spread = values - center
    second = jnp.mean(spread * spread, axis=-1, keepdims=True)
    return spread * lax.rsqrt(second + EPS) * norm_gain + norm_bias


def merge_pair(first_part, second_part):
    first_max, first_sum, first_out = first_part
    second_max, second_sum, second_out = second_part
    joint_max = jnp.maximum(first_max, second_max)
    first_scale = jnp.exp(first_max - joint_max)
    second_scale = jnp.exp(second_max - joint_max)
    return (
        joint_max,
        first_sum * first_scale + second_sum * second_scale,
        first_out * first_scale[..., None] + second_out * second_scale[..., None],
    )


def partial_attention(queries, keys_here, values_here, visible):
    scores = jnp.einsum(
        "rthe,rphe->rthp", queries, keys_here, preferred_element_type=jnp.float32
    ) * HDIM ** (-0.5)
    highest = jnp.max(jnp.where(visible, scores, NEG), axis=-1)
    weights = jnp.exp(jnp.where(visible, scores - highest[..., None], NEG)).astype(jnp.bfloat16)
    totals = jnp.sum(weights.astype(jnp.float32), axis=-1)
    blended = jnp.einsum(
        "rthp,rphe->rthe", weights, values_here, preferred_element_type=jnp.float32
    )
    return (highest, totals, blended)


def merge_rows(mine, theirs, width):
    top, total, out = mine
    o_top, o_total, o_out = theirs
    joint = jnp.maximum(top, o_top)
    scale = jnp.exp(top - joint)
    o_scale = jnp.exp(o_top - joint)
    out = out * jnp.repeat(scale, width, axis=1) + o_out * jnp.repeat(o_scale, width, axis=1)
    return (joint, total * scale + o_total * o_scale, out)


def exchange(stats, pairs):
    top, total, out = stats
    rows, heads = top.shape
    lanes = out.shape[1]
    flat = jnp.concatenate([top, total], axis=1).reshape(-1)
    fill = (-flat.size) % lanes
    flat = jnp.pad(flat, (0, fill)).reshape(-1, lanes)
    other = lax.ppermute(jnp.concatenate([out, flat], axis=0), "seq", pairs)
    o_out = other[:rows]
    o_flat = other[rows:].reshape(-1)[: rows * 2 * heads].reshape(rows, 2 * heads)
    return (o_flat[:, :heads], o_flat[:, heads:], o_out)


def pick(flag, when_set, when_clear):
    return jax.tree.map(lambda a, b: jnp.where(flag, a, b), when_set, when_clear)


def seq_attend(stats, width):
    n_seq = lax.axis_size("seq")
    me = lax.axis_index("seq")
    rows = stats[2].shape[0]
    bit = 1
    scatter_bits = []
    while bit < n_seq and rows % 16 == 0 and len(scatter_bits) < 2:
        half = rows // 2
        upper = (me // bit) % 2 == 1
        low = jax.tree.map(lambda a: a[:half], stats)
        high = jax.tree.map(lambda a: a[half:], stats)
        keep = pick(upper, high, low)
        send = pick(upper, low, high)
        other = exchange(send, [(i, i ^ bit) for i in range(n_seq)])
        stats = merge_rows(keep, other, width)
        scatter_bits.append(bit)
        rows = half
        bit *= 2
    while bit < n_seq:
        other = exchange(stats, [(i, i ^ bit) for i in range(n_seq)])
        stats = merge_rows(stats, other, width)
        bit *= 2
    top, total, out = stats
    attended = (out / jnp.repeat(total, width, axis=1)).astype(jnp.bfloat16)
    n_head = lax.axis_size("head")
    if 2 ** len(scatter_bits) == n_head:
        return send_to_owners(attended, scatter_bits)
    for bit in reversed(scatter_bits):
        upper = (me // bit) % 2 == 1
        other = lax.ppermute(attended, "seq", [(i, i ^ bit) for i in range(n_seq)])
        attended = jnp.where(
            upper,
            jnp.concatenate([other, attended], axis=0),
            jnp.concatenate([attended, other], axis=0),
        )
    return attended


def send_to_owners(chunk, scatter_bits):
    n_seq = lax.axis_size("seq")
    n_head = lax.axis_size("head")
    depth = len(scatter_bits)

    def block_of(s):
        return sum(((s // b) % 2) << (depth - 1 - j) for j, b in enumerate(scatter_bits))

    def with_block(s, c):
        for j, b in enumerate(scatter_bits):
            want = (c >> (depth - 1 - j)) % 2
            s = s - ((s // b) % 2) * b + want * b
        return s

    received = []
    for k in range(n_head):
        pairs = [
            (s * n_head + h, with_block(s, (h + k) % n_head) * n_head + block_of(s))
            for s in range(n_seq)
            for h in range(n_head)
        ]
        received.append(lax.ppermute(chunk, ("seq", "head"), pairs))
    stacked = jnp.stack(received)
    me = lax.axis_index("seq")
    mine = sum(((me // b) % 2) << (depth - 1 - j) for j, b in enumerate(scatter_bits))
    order = (mine - jnp.arange(n_head)) % n_head
    picked = jnp.take(stacked, order, axis=0)
    return jnp.concatenate([picked[h] for h in range(n_head)], axis=1)


def head_gather(x):
    n_head = lax.axis_size("head")
    me = lax.axis_index("head")
    parts = [x]
    for shift in range(1, n_head):
        parts.append(lax.ppermute(x, "head", [(i, (i + shift) % n_head) for i in range(n_head)]))
    stacked = jnp.stack(parts)
    order = (me - jnp.arange(n_head)) % n_head
    return jnp.take(stacked, order, axis=0)

def on_device(
    tokens,
    cache_keys,
    cache_values,
    held_states,
    recompute_pos,
    cache_len,
    new_prompt,
    w_qkv,
    qkv_bias,
    w_out,
    out_bias,
    attn_gain,
    attn_shift,
    w_up,
    up_bias,
    w_down,
    down_bias,
    ffn_gain,
    ffn_shift,
):
    local_width = w_qkv.shape[2]
    local_heads = local_width // HDIM
    requests = cache_keys.shape[0]
    block_len = cache_keys.shape[1]
    own_rows = tokens.shape[0]
    steps_count = tokens.shape[1]
    block_rows = head_gather(tokens).reshape((-1,) + tokens.shape[1:])
    triple = (
        jnp.einsum("rtd,kdc->rtkc", block_rows, w_qkv, preferred_element_type=jnp.float32)
        + qkv_bias
    )
    triple = triple.astype(jnp.bfloat16).reshape(
        block_rows.shape[0], block_rows.shape[1], 3 * local_width
    )
    gathered = jnp.concatenate([triple, block_rows], axis=2)
    head_shape = (requests, steps_count, local_heads, HDIM)
    queries = gathered[:, :, :local_width].reshape(head_shape)
    new_keys = gathered[:, :, local_width : 2 * local_width].reshape(head_shape)
    new_values = gathered[:, :, 2 * local_width : 3 * local_width].reshape(head_shape)
    fresh_keys = (
        jnp.einsum("rjd,dc->rjc", held_states, w_qkv[1], preferred_element_type=jnp.float32)
        + qkv_bias[1]
    ).astype(jnp.bfloat16)
    offset_pos = lax.axis_index("seq") * block_len
    positions = jnp.arange(block_len, dtype=jnp.int32)
    matches = (recompute_pos - offset_pos)[:, :, None] == positions[None, None, :]
    placed = jnp.einsum(
        "rjp,rjc->rpc", matches.astype(jnp.bfloat16), fresh_keys, preferred_element_type=jnp.float32
    ).astype(jnp.bfloat16)
    replaced = jnp.any(matches, axis=1)
    keys_here = jnp.where(replaced[:, :, None], placed, cache_keys).reshape(
        requests, block_len, local_heads, HDIM
    )
    values_here = cache_values.reshape(requests, block_len, local_heads, HDIM)
    visible = ((offset_pos + positions)[None, :] < cache_len[:, None]) & (new_prompt[:, None] == 0)
    block_max, block_sum, block_out = partial_attention(
        queries, keys_here, values_here, visible[:, None, None, :]
    )
    order_t = jnp.arange(steps_count, dtype=jnp.int32)
    causal = (order_t[:, None] >= order_t[None, :])[None, :, None, :]
    new_max, new_sum, new_out = partial_attention(queries, new_keys, new_values, causal)
    rows = requests * steps_count
    flat = lambda m, s, o: (m.reshape(rows, local_heads), s.reshape(rows, local_heads), o.reshape(rows, local_width))
    cache_part = flat(block_max, block_sum, block_out)
    new_part = flat(new_max, new_sum, new_out)
    first = lax.axis_index("seq") == 0
    stats = pick(first, merge_rows(cache_part, new_part, HDIM), cache_part)
    own_attended = seq_attend(stats, HDIM).reshape(own_rows, steps_count, -1)
    n_seq = lax.axis_size("seq")
    core = lax.axis_index("seq") % 2
    pair = [(i, i ^ 1) for i in range(n_seq)]
    d_half = w_out.shape[1] // 2
    w_out_half = lax.dynamic_slice_in_dim(w_out, core * d_half, d_half, 1)
    ffw_half = w_up.shape[1] // 2
    bias_half = lax.dynamic_slice_in_dim(up_bias, core * ffw_half, ffw_half, 0)
    bias_hi = lax.reduce_precision(bias_half, exponent_bits=8, mantissa_bits=7)
    rest = bias_half - bias_hi
    bias_mid = lax.reduce_precision(rest, exponent_bits=8, mantissa_bits=7)
    bias_lo = rest - bias_mid
    pieces = jnp.stack([bias_hi, bias_mid, bias_lo]).astype(jnp.bfloat16)
    pieces = jnp.pad(pieces, ((0, 5), (0, 0)))
    up_rows = w_up.shape[0]
    out_rows = w_out_half.size // ffw_half
    w_up_all = lax.all_gather(
        jnp.concatenate(
            [
                lax.dynamic_slice_in_dim(w_up, core * ffw_half, ffw_half, 1),
                pieces,
                w_out_half.reshape(out_rows, ffw_half),
            ],
            axis=0,
        ),
        "head",
        axis=0,
    )
    got = w_up_all[:, up_rows : up_rows + 3].astype(jnp.float32)
    up_bias_all = got[:, 0] + got[:, 1] + got[:, 2]
    w_out_all = w_up_all[:, up_rows + 8 :].reshape(-1, d_half)
    w_up_all = w_up_all[:, :up_rows]
    w_down_all = lax.all_gather(
        lax.dynamic_slice_in_dim(w_down, core * ffw_half, ffw_half, 0), "head", axis=0
    )
    projected = jnp.einsum(
        "rtc,cd->rtd", own_attended, w_out_all, preferred_element_type=jnp.float32
    )
    other_half = lax.ppermute(projected, "seq", pair)
    projected = jnp.where(
        core == 1,
        jnp.concatenate([other_half, projected], axis=2),
        jnp.concatenate([projected, other_half], axis=2),
    )
    normed = layer_norm(
        tokens.astype(jnp.float32) + projected + out_bias, attn_gain, attn_shift
    ).astype(jnp.bfloat16)
    hidden = jax.nn.gelu(
        jnp.einsum("rtd,hdf->rthf", normed, w_up_all, preferred_element_type=jnp.float32)
        + up_bias_all,
        approximate=False,
    ).astype(jnp.bfloat16)
    lowered = jnp.einsum("rthf,hfd->rtd", hidden, w_down_all, preferred_element_type=jnp.float32)
    lowered = lowered + lax.ppermute(lowered, "seq", pair)
    return layer_norm(normed.astype(jnp.float32) + lowered + down_bias, ffn_gain, ffn_shift).astype(
        jnp.bfloat16
    )


def solution(mesh):
    placed = (
        P("head", None, None),
        P(None, "seq", "head"),
        P(None, "seq", "head"),
        P(None, "seq", None),
        P(None, "seq"),
        P(),
        P(),
        P(None, None, "head"),
        P(None, "head"),
        P("head", None),
        P(),
        P(),
        P(),
        P(None, "head"),
        P("head"),
        P("head", None),
        P(),
        P(),
        P(),
    )
    return jax.shard_map(
        on_device, mesh=mesh, in_specs=placed, out_specs=P("head", None, None), check_vma=False
    )
```

```python
import jax
import jax.numpy as jnp
from jax import lax
from jax.sharding import PartitionSpec as P

HDIM = 64


NEG = -1e30
EPS = 1e-05


def layer_norm(values, norm_gain, norm_bias):
    center = jnp.mean(values, axis=-1, keepdims=True)
    spread = values - center
    second = jnp.mean(spread * spread, axis=-1, keepdims=True)
    return spread * lax.rsqrt(second + EPS) * norm_gain + norm_bias


def merge_pair(first_part, second_part):
    first_max, first_sum, first_out = first_part
    second_max, second_sum, second_out = second_part
    joint_max = jnp.maximum(first_max, second_max)
    first_scale = jnp.exp(first_max - joint_max)
    second_scale = jnp.exp(second_max - joint_max)
    return (
        joint_max,
        first_sum * first_scale + second_sum * second_scale,
        first_out * first_scale[..., None] + second_out * second_scale[..., None],
    )


def partial_attention(queries, keys_here, values_here, visible):
    scores = jnp.einsum(
        "rthe,rphe->rthp", queries, keys_here, preferred_element_type=jnp.float32
    ) * HDIM ** (-0.5)
    highest = jnp.max(jnp.where(visible, scores, NEG), axis=-1)
    weights = jnp.exp(jnp.where(visible, scores - highest[..., None], NEG)).astype(jnp.bfloat16)
    totals = jnp.sum(weights.astype(jnp.float32), axis=-1)
    blended = jnp.einsum(
        "rthp,rphe->rthe", weights, values_here, preferred_element_type=jnp.float32
    )
    return (highest, totals, blended)


def merge_rows(mine, theirs, width):
    top, total, out = mine
    o_top, o_total, o_out = theirs
    joint = jnp.maximum(top, o_top)
    scale = jnp.exp(top - joint)
    o_scale = jnp.exp(o_top - joint)
    out = out * jnp.repeat(scale, width, axis=1) + o_out * jnp.repeat(o_scale, width, axis=1)
    return (joint, total * scale + o_total * o_scale, out)


def exchange(stats, pairs):
    top, total, out = stats
    rows, heads = top.shape
    lanes = out.shape[1]
    flat = jnp.concatenate([top, total], axis=1).reshape(-1)
    fill = (-flat.size) % lanes
    flat = jnp.pad(flat, (0, fill)).reshape(-1, lanes)
    other = lax.ppermute(jnp.concatenate([out, flat], axis=0), "seq", pairs)
    o_out = other[:rows]
    o_flat = other[rows:].reshape(-1)[: rows * 2 * heads].reshape(rows, 2 * heads)
    return (o_flat[:, :heads], o_flat[:, heads:], o_out)


def pick(flag, when_set, when_clear):
    return jax.tree.map(lambda a, b: jnp.where(flag, a, b), when_set, when_clear)


def seq_attend(stats, width):
    n_seq = lax.axis_size("seq")
    me = lax.axis_index("seq")
    rows = stats[2].shape[0]
    bit = 1
    scatter_bits = []
    while bit < n_seq and rows % 16 == 0 and len(scatter_bits) < 2:
        half = rows // 2
        upper = (me // bit) % 2 == 1
        low = jax.tree.map(lambda a: a[:half], stats)
        high = jax.tree.map(lambda a: a[half:], stats)
        keep = pick(upper, high, low)
        send = pick(upper, low, high)
        other = exchange(send, [(i, i ^ bit) for i in range(n_seq)])
        stats = merge_rows(keep, other, width)
        scatter_bits.append(bit)
        rows = half
        bit *= 2
    while bit < n_seq:
        other = exchange(stats, [(i, i ^ bit) for i in range(n_seq)])
        stats = merge_rows(stats, other, width)
        bit *= 2
    top, total, out = stats
    attended = (out / jnp.repeat(total, width, axis=1)).astype(jnp.bfloat16)
    for bit in reversed(scatter_bits):
        upper = (me // bit) % 2 == 1
        other = lax.ppermute(attended, "seq", [(i, i ^ bit) for i in range(n_seq)])
        attended = jnp.where(
            upper,
            jnp.concatenate([other, attended], axis=0),
            jnp.concatenate([attended, other], axis=0),
        )
    return attended


def head_gather(x):
    n_head = lax.axis_size("head")
    me = lax.axis_index("head")
    parts = [x]
    for shift in range(1, n_head):
        parts.append(lax.ppermute(x, "head", [(i, (i + shift) % n_head) for i in range(n_head)]))
    stacked = jnp.stack(parts)
    order = (me - jnp.arange(n_head)) % n_head
    return jnp.take(stacked, order, axis=0)

def on_device(
    tokens,
    cache_keys,
    cache_values,
    held_states,
    recompute_pos,
    cache_len,
    new_prompt,
    w_qkv,
    qkv_bias,
    w_out,
    out_bias,
    attn_gain,
    attn_shift,
    w_up,
    up_bias,
    w_down,
    down_bias,
    ffn_gain,
    ffn_shift,
):
    local_width = w_qkv.shape[2]
    local_heads = local_width // HDIM
    requests = cache_keys.shape[0]
    block_len = cache_keys.shape[1]
    own_rows = tokens.shape[0]
    steps_count = tokens.shape[1]
    block_rows = head_gather(tokens).reshape((-1,) + tokens.shape[1:])
    triple = (
        jnp.einsum("rtd,kdc->rtkc", block_rows, w_qkv, preferred_element_type=jnp.float32)
        + qkv_bias
    )
    triple = triple.astype(jnp.bfloat16).reshape(
        block_rows.shape[0], block_rows.shape[1], 3 * local_width
    )
    gathered = jnp.concatenate([triple, block_rows], axis=2)
    head_shape = (requests, steps_count, local_heads, HDIM)
    queries = gathered[:, :, :local_width].reshape(head_shape)
    new_keys = gathered[:, :, local_width : 2 * local_width].reshape(head_shape)
    new_values = gathered[:, :, 2 * local_width : 3 * local_width].reshape(head_shape)
    fresh_keys = (
        jnp.einsum("rjd,dc->rjc", held_states, w_qkv[1], preferred_element_type=jnp.float32)
        + qkv_bias[1]
    ).astype(jnp.bfloat16)
    offset_pos = lax.axis_index("seq") * block_len
    positions = jnp.arange(block_len, dtype=jnp.int32)
    matches = (recompute_pos - offset_pos)[:, :, None] == positions[None, None, :]
    placed = jnp.einsum(
        "rjp,rjc->rpc", matches.astype(jnp.bfloat16), fresh_keys, preferred_element_type=jnp.float32
    ).astype(jnp.bfloat16)
    replaced = jnp.any(matches, axis=1)
    keys_here = jnp.where(replaced[:, :, None], placed, cache_keys).reshape(
        requests, block_len, local_heads, HDIM
    )
    values_here = cache_values.reshape(requests, block_len, local_heads, HDIM)
    visible = ((offset_pos + positions)[None, :] < cache_len[:, None]) & (new_prompt[:, None] == 0)
    block_max, block_sum, block_out = partial_attention(
        queries, keys_here, values_here, visible[:, None, None, :]
    )
    order_t = jnp.arange(steps_count, dtype=jnp.int32)
    causal = (order_t[:, None] >= order_t[None, :])[None, :, None, :]
    new_max, new_sum, new_out = partial_attention(queries, new_keys, new_values, causal)
    rows = requests * steps_count
    flat = lambda m, s, o: (m.reshape(rows, local_heads), s.reshape(rows, local_heads), o.reshape(rows, local_width))
    cache_part = flat(block_max, block_sum, block_out)
    new_part = flat(new_max, new_sum, new_out)
    first = lax.axis_index("seq") == 0
    stats = pick(first, merge_rows(cache_part, new_part, HDIM), cache_part)
    attended = seq_attend(stats, HDIM).reshape(requests, steps_count, local_width)
    n_seq = lax.axis_size("seq")
    core = lax.axis_index("seq") % 2
    pair = [(i, i ^ 1) for i in range(n_seq)]
    ffw_half = w_up.shape[1] // 2
    bias_half = lax.dynamic_slice_in_dim(up_bias, core * ffw_half, ffw_half, 0)
    bias_hi = lax.reduce_precision(bias_half, exponent_bits=8, mantissa_bits=7)
    rest = bias_half - bias_hi
    bias_mid = lax.reduce_precision(rest, exponent_bits=8, mantissa_bits=7)
    bias_lo = rest - bias_mid
    pieces = jnp.stack([bias_hi, bias_mid, bias_lo]).astype(jnp.bfloat16)
    pieces = jnp.pad(pieces, ((0, 5), (0, 0)))
    up_rows = w_up.shape[0]
    w_up_all = lax.all_gather(
        jnp.concatenate(
            [lax.dynamic_slice_in_dim(w_up, core * ffw_half, ffw_half, 1), pieces], axis=0
        ),
        "head",
        axis=0,
    )
    got = w_up_all[:, up_rows : up_rows + 3].astype(jnp.float32)
    up_bias_all = got[:, 0] + got[:, 1] + got[:, 2]
    w_up_all = w_up_all[:, :up_rows]
    w_down_all = lax.all_gather(
        jnp.concatenate([lax.dynamic_slice_in_dim(w_down, core * ffw_half, ffw_half, 0), w_out]),
        "head",
        axis=0,
    )
    w_out_all = w_down_all[:, ffw_half:].reshape(-1, w_out.shape[1])
    w_down_all = w_down_all[:, :ffw_half]
    own_attended = lax.all_to_all(attended, "head", 0, 2, tiled=True)
    projected = jnp.einsum(
        "rtc,cd->rtd", own_attended, w_out_all, preferred_element_type=jnp.float32
    )
    normed = layer_norm(
        tokens.astype(jnp.float32) + projected + out_bias, attn_gain, attn_shift
    ).astype(jnp.bfloat16)
    hidden = jax.nn.gelu(
        jnp.einsum("rtd,hdf->rthf", normed, w_up_all, preferred_element_type=jnp.float32)
        + up_bias_all,
        approximate=False,
    ).astype(jnp.bfloat16)
    lowered = jnp.einsum("rthf,hfd->rtd", hidden, w_down_all, preferred_element_type=jnp.float32)
    lowered = lowered + lax.ppermute(lowered, "seq", pair)
    return layer_norm(normed.astype(jnp.float32) + lowered + down_bias, ffn_gain, ffn_shift).astype(
        jnp.bfloat16
    )


def solution(mesh):
    placed = (
        P("head", None, None),
        P(None, "seq", "head"),
        P(None, "seq", "head"),
        P(None, "seq", None),
        P(None, "seq"),
        P(),
        P(),
        P(None, None, "head"),
        P(None, "head"),
        P("head", None),
        P(),
        P(),
        P(),
        P(None, "head"),
        P("head"),
        P("head", None),
        P(),
        P(),
        P(),
    )
    return jax.shard_map(
        on_device, mesh=mesh, in_specs=placed, out_specs=P("head", None, None), check_vma=False
    )
```

```python
import jax
import jax.numpy as jnp
from jax import lax
from jax.sharding import PartitionSpec as P

HDIM = 64


NEG = -1e30
EPS = 1e-05


def layer_norm(values, norm_gain, norm_bias):
    center = jnp.mean(values, axis=-1, keepdims=True)
    spread = values - center
    second = jnp.mean(spread * spread, axis=-1, keepdims=True)
    return spread * lax.rsqrt(second + EPS) * norm_gain + norm_bias


def merge_pair(first_part, second_part):
    first_max, first_sum, first_out = first_part
    second_max, second_sum, second_out = second_part
    joint_max = jnp.maximum(first_max, second_max)
    first_scale = jnp.exp(first_max - joint_max)
    second_scale = jnp.exp(second_max - joint_max)
    return (
        joint_max,
        first_sum * first_scale + second_sum * second_scale,
        first_out * first_scale[..., None] + second_out * second_scale[..., None],
    )


def partial_attention(queries, keys_here, values_here, visible):
    scores = jnp.einsum(
        "rthe,rphe->rthp", queries, keys_here, preferred_element_type=jnp.float32
    ) * HDIM ** (-0.5)
    highest = jnp.max(jnp.where(visible, scores, NEG), axis=-1)
    weights = jnp.exp(jnp.where(visible, scores - highest[..., None], NEG)).astype(jnp.bfloat16)
    totals = jnp.sum(weights.astype(jnp.float32), axis=-1)
    blended = jnp.einsum(
        "rthp,rphe->rthe", weights, values_here, preferred_element_type=jnp.float32
    )
    return (highest, totals, blended)


def merge_rows(mine, theirs, width):
    top, total, out = mine
    o_top, o_total, o_out = theirs
    joint = jnp.maximum(top, o_top)
    scale = jnp.exp(top - joint)
    o_scale = jnp.exp(o_top - joint)
    out = out * jnp.repeat(scale, width, axis=1) + o_out * jnp.repeat(o_scale, width, axis=1)
    return (joint, total * scale + o_total * o_scale, out)


def exchange(stats, pairs):
    top, total, out = stats
    rows, heads = top.shape
    lanes = out.shape[1]
    flat = jnp.concatenate([top, total], axis=1).reshape(-1)
    fill = (-flat.size) % lanes
    flat = jnp.pad(flat, (0, fill)).reshape(-1, lanes)
    other = lax.ppermute(jnp.concatenate([out, flat], axis=0), "seq", pairs)
    o_out = other[:rows]
    o_flat = other[rows:].reshape(-1)[: rows * 2 * heads].reshape(rows, 2 * heads)
    return (o_flat[:, :heads], o_flat[:, heads:], o_out)


def pick(flag, when_set, when_clear):
    return jax.tree.map(lambda a, b: jnp.where(flag, a, b), when_set, when_clear)


def seq_attend(stats, width):
    n_seq = lax.axis_size("seq")
    me = lax.axis_index("seq")
    rows = stats[2].shape[0]
    bit = 1
    scatter_bits = []
    while bit < n_seq and rows % 16 == 0 and len(scatter_bits) < 2:
        half = rows // 2
        upper = (me // bit) % 2 == 1
        low = jax.tree.map(lambda a: a[:half], stats)
        high = jax.tree.map(lambda a: a[half:], stats)
        keep = pick(upper, high, low)
        send = pick(upper, low, high)
        other = exchange(send, [(i, i ^ bit) for i in range(n_seq)])
        stats = merge_rows(keep, other, width)
        scatter_bits.append(bit)
        rows = half
        bit *= 2
    while bit < n_seq:
        if bit * 4 == n_seq:
            group = [stats]
            for k in (1, 2, 3):
                group.append(exchange(stats, [(i, i ^ (k * bit)) for i in range(n_seq)]))
            stacked = jax.tree.map(lambda *a: jnp.stack(a), *group)
            mine = (me // bit) % 4
            block = lambda j: jax.tree.map(lambda a: a[mine ^ j], stacked)
            low = merge_rows(block(0), block(1), width)
            high = merge_rows(block(2), block(3), width)
            stats = merge_rows(low, high, width)
            break
        other = exchange(stats, [(i, i ^ bit) for i in range(n_seq)])
        stats = merge_rows(stats, other, width)
        bit *= 2
    top, total, out = stats
    attended = (out / jnp.repeat(total, width, axis=1)).astype(jnp.bfloat16)
    for bit in reversed(scatter_bits):
        upper = (me // bit) % 2 == 1
        other = lax.ppermute(attended, "seq", [(i, i ^ bit) for i in range(n_seq)])
        attended = jnp.where(
            upper,
            jnp.concatenate([other, attended], axis=0),
            jnp.concatenate([attended, other], axis=0),
        )
    return attended


def head_gather(x):
    n_head = lax.axis_size("head")
    me = lax.axis_index("head")
    parts = [x]
    for shift in range(1, n_head):
        parts.append(lax.ppermute(x, "head", [(i, (i + shift) % n_head) for i in range(n_head)]))
    stacked = jnp.stack(parts)
    order = (me - jnp.arange(n_head)) % n_head
    return jnp.take(stacked, order, axis=0)

def on_device(
    tokens,
    cache_keys,
    cache_values,
    held_states,
    recompute_pos,
    cache_len,
    new_prompt,
    w_qkv,
    qkv_bias,
    w_out,
    out_bias,
    attn_gain,
    attn_shift,
    w_up,
    up_bias,
    w_down,
    down_bias,
    ffn_gain,
    ffn_shift,
):
    local_width = w_qkv.shape[2]
    local_heads = local_width // HDIM
    requests = cache_keys.shape[0]
    block_len = cache_keys.shape[1]
    own_rows = tokens.shape[0]
    steps_count = tokens.shape[1]
    block_rows = head_gather(tokens).reshape((-1,) + tokens.shape[1:])
    triple = (
        jnp.einsum("rtd,kdc->rtkc", block_rows, w_qkv, preferred_element_type=jnp.float32)
        + qkv_bias
    )
    triple = triple.astype(jnp.bfloat16).reshape(
        block_rows.shape[0], block_rows.shape[1], 3 * local_width
    )
    gathered = jnp.concatenate([triple, block_rows], axis=2)
    head_shape = (requests, steps_count, local_heads, HDIM)
    queries = gathered[:, :, :local_width].reshape(head_shape)
    new_keys = gathered[:, :, local_width : 2 * local_width].reshape(head_shape)
    new_values = gathered[:, :, 2 * local_width : 3 * local_width].reshape(head_shape)
    fresh_keys = (
        jnp.einsum("rjd,dc->rjc", held_states, w_qkv[1], preferred_element_type=jnp.float32)
        + qkv_bias[1]
    ).astype(jnp.bfloat16)
    offset_pos = lax.axis_index("seq") * block_len
    positions = jnp.arange(block_len, dtype=jnp.int32)
    matches = (recompute_pos - offset_pos)[:, :, None] == positions[None, None, :]
    placed = jnp.einsum(
        "rjp,rjc->rpc", matches.astype(jnp.bfloat16), fresh_keys, preferred_element_type=jnp.float32
    ).astype(jnp.bfloat16)
    replaced = jnp.any(matches, axis=1)
    keys_here = jnp.where(replaced[:, :, None], placed, cache_keys).reshape(
        requests, block_len, local_heads, HDIM
    )
    values_here = cache_values.reshape(requests, block_len, local_heads, HDIM)
    visible = ((offset_pos + positions)[None, :] < cache_len[:, None]) & (new_prompt[:, None] == 0)
    block_max, block_sum, block_out = partial_attention(
        queries, keys_here, values_here, visible[:, None, None, :]
    )
    order_t = jnp.arange(steps_count, dtype=jnp.int32)
    causal = (order_t[:, None] >= order_t[None, :])[None, :, None, :]
    new_max, new_sum, new_out = partial_attention(queries, new_keys, new_values, causal)
    rows = requests * steps_count
    flat = lambda m, s, o: (m.reshape(rows, local_heads), s.reshape(rows, local_heads), o.reshape(rows, local_width))
    cache_part = flat(block_max, block_sum, block_out)
    new_part = flat(new_max, new_sum, new_out)
    first = lax.axis_index("seq") == 0
    stats = pick(first, merge_rows(cache_part, new_part, HDIM), cache_part)
    attended = seq_attend(stats, HDIM).reshape(requests, steps_count, local_width)
    n_seq = lax.axis_size("seq")
    core = lax.axis_index("seq") % 2
    pair = [(i, i ^ 1) for i in range(n_seq)]
    ffw_half = w_up.shape[1] // 2
    bias_half = lax.dynamic_slice_in_dim(up_bias, core * ffw_half, ffw_half, 0)
    bias_hi = lax.reduce_precision(bias_half, exponent_bits=8, mantissa_bits=7)
    rest = bias_half - bias_hi
    bias_mid = lax.reduce_precision(rest, exponent_bits=8, mantissa_bits=7)
    bias_lo = rest - bias_mid
    pieces = jnp.stack([bias_hi, bias_mid, bias_lo]).astype(jnp.bfloat16)
    pieces = jnp.pad(pieces, ((0, 5), (0, 0)))
    up_rows = w_up.shape[0]
    w_up_all = lax.all_gather(
        jnp.concatenate(
            [lax.dynamic_slice_in_dim(w_up, core * ffw_half, ffw_half, 1), pieces], axis=0
        ),
        "head",
        axis=0,
    )
    got = w_up_all[:, up_rows : up_rows + 3].astype(jnp.float32)
    up_bias_all = got[:, 0] + got[:, 1] + got[:, 2]
    w_up_all = w_up_all[:, :up_rows]
    w_down_all = lax.all_gather(
        jnp.concatenate([lax.dynamic_slice_in_dim(w_down, core * ffw_half, ffw_half, 0), w_out]),
        "head",
        axis=0,
    )
    w_out_all = w_down_all[:, ffw_half:].reshape(-1, w_out.shape[1])
    w_down_all = w_down_all[:, :ffw_half]
    own_attended = lax.all_to_all(attended, "head", 0, 2, tiled=True)
    projected = jnp.einsum(
        "rtc,cd->rtd", own_attended, w_out_all, preferred_element_type=jnp.float32
    )
    normed = layer_norm(
        tokens.astype(jnp.float32) + projected + out_bias, attn_gain, attn_shift
    ).astype(jnp.bfloat16)
    hidden = jax.nn.gelu(
        jnp.einsum("rtd,hdf->rthf", normed, w_up_all, preferred_element_type=jnp.float32)
        + up_bias_all,
        approximate=False,
    ).astype(jnp.bfloat16)
    lowered = jnp.einsum("rthf,hfd->rtd", hidden, w_down_all, preferred_element_type=jnp.float32)
    lowered = lowered + lax.ppermute(lowered, "seq", pair)
    return layer_norm(normed.astype(jnp.float32) + lowered + down_bias, ffn_gain, ffn_shift).astype(
        jnp.bfloat16
    )


def solution(mesh):
    placed = (
        P("head", None, None),
        P(None, "seq", "head"),
        P(None, "seq", "head"),
        P(None, "seq", None),
        P(None, "seq"),
        P(),
        P(),
        P(None, None, "head"),
        P(None, "head"),
        P("head", None),
        P(),
        P(),
        P(),
        P(None, "head"),
        P("head"),
        P("head", None),
        P(),
        P(),
        P(),
    )
    return jax.shard_map(
        on_device, mesh=mesh, in_specs=placed, out_specs=P("head", None, None), check_vma=False
    )
```

```python
import jax
import jax.numpy as jnp
from jax import lax
from jax.sharding import PartitionSpec as P

HDIM = 64


NEG = -1e30
EPS = 1e-05


def layer_norm(values, norm_gain, norm_bias):
    center = jnp.mean(values, axis=-1, keepdims=True)
    spread = values - center
    second = jnp.mean(spread * spread, axis=-1, keepdims=True)
    return spread * lax.rsqrt(second + EPS) * norm_gain + norm_bias


def merge_pair(first_part, second_part):
    first_max, first_sum, first_out = first_part
    second_max, second_sum, second_out = second_part
    joint_max = jnp.maximum(first_max, second_max)
    first_scale = jnp.exp(first_max - joint_max)
    second_scale = jnp.exp(second_max - joint_max)
    return (
        joint_max,
        first_sum * first_scale + second_sum * second_scale,
        first_out * first_scale[..., None] + second_out * second_scale[..., None],
    )


def partial_attention(queries, keys_here, values_here, visible):
    scores = jnp.einsum(
        "rthe,rphe->rthp", queries, keys_here, preferred_element_type=jnp.float32
    ) * HDIM ** (-0.5)
    highest = jnp.max(jnp.where(visible, scores, NEG), axis=-1)
    weights = jnp.exp(jnp.where(visible, scores - highest[..., None], NEG)).astype(jnp.bfloat16)
    totals = jnp.sum(weights.astype(jnp.float32), axis=-1)
    blended = jnp.einsum(
        "rthp,rphe->rthe", weights, values_here, preferred_element_type=jnp.float32
    )
    return (highest, totals, blended)


def merge_rows(mine, theirs, width):
    top, total, out = mine
    o_top, o_total, o_out = theirs
    joint = jnp.maximum(top, o_top)
    scale = jnp.exp(top - joint)
    o_scale = jnp.exp(o_top - joint)
    out = out * jnp.repeat(scale, width, axis=1) + o_out * jnp.repeat(o_scale, width, axis=1)
    return (joint, total * scale + o_total * o_scale, out)


def exchange(stats, pairs):
    top, total, out = stats
    rows, heads = top.shape
    lanes = out.shape[1]
    flat = jnp.concatenate([top, total], axis=1).reshape(-1)
    fill = (-flat.size) % lanes
    flat = jnp.pad(flat, (0, fill)).reshape(-1, lanes)
    other = lax.ppermute(jnp.concatenate([out, flat], axis=0), "seq", pairs)
    o_out = other[:rows]
    o_flat = other[rows:].reshape(-1)[: rows * 2 * heads].reshape(rows, 2 * heads)
    return (o_flat[:, :heads], o_flat[:, heads:], o_out)


def pick(flag, when_set, when_clear):
    return jax.tree.map(lambda a, b: jnp.where(flag, a, b), when_set, when_clear)


def seq_attend(stats, width):
    n_seq = lax.axis_size("seq")
    me = lax.axis_index("seq")
    rows = stats[2].shape[0]
    bit = 1
    scatter_bits = []
    while bit < n_seq and rows % 16 == 0 and len(scatter_bits) < 2:
        half = rows // 2
        upper = (me // bit) % 2 == 1
        low = jax.tree.map(lambda a: a[:half], stats)
        high = jax.tree.map(lambda a: a[half:], stats)
        keep = pick(upper, high, low)
        send = pick(upper, low, high)
        other = exchange(send, [(i, i ^ bit) for i in range(n_seq)])
        stats = merge_rows(keep, other, width)
        scatter_bits.append(bit)
        rows = half
        bit *= 2
    while bit < n_seq:
        if bit * 4 == n_seq:
            group = [stats]
            for k in (1, 2, 3):
                group.append(exchange(stats, [(i, i ^ (k * bit)) for i in range(n_seq)]))
            stacked = jax.tree.map(lambda *a: jnp.stack(a), *group)
            mine = (me // bit) % 4
            block = lambda j: jax.tree.map(lambda a: a[mine ^ j], stacked)
            low = merge_rows(block(0), block(1), width)
            high = merge_rows(block(2), block(3), width)
            stats = merge_rows(low, high, width)
            break
        other = exchange(stats, [(i, i ^ bit) for i in range(n_seq)])
        stats = merge_rows(stats, other, width)
        bit *= 2
    top, total, out = stats
    attended = (out / jnp.repeat(total, width, axis=1)).astype(jnp.bfloat16)
    for bit in reversed(scatter_bits):
        upper = (me // bit) % 2 == 1
        other = lax.ppermute(attended, "seq", [(i, i ^ bit) for i in range(n_seq)])
        attended = jnp.where(
            upper,
            jnp.concatenate([other, attended], axis=0),
            jnp.concatenate([attended, other], axis=0),
        )
    return attended


def head_gather(x):
    n_head = lax.axis_size("head")
    me = lax.axis_index("head")
    parts = [x]
    for shift in range(1, n_head):
        parts.append(lax.ppermute(x, "head", [(i, (i + shift) % n_head) for i in range(n_head)]))
    stacked = jnp.stack(parts)
    order = (me - jnp.arange(n_head)) % n_head
    return jnp.take(stacked, order, axis=0)

def on_device(
    tokens,
    cache_keys,
    cache_values,
    held_states,
    recompute_pos,
    cache_len,
    new_prompt,
    w_qkv,
    qkv_bias,
    w_out,
    out_bias,
    attn_gain,
    attn_shift,
    w_up,
    up_bias,
    w_down,
    down_bias,
    ffn_gain,
    ffn_shift,
):
    local_width = w_qkv.shape[2]
    local_heads = local_width // HDIM
    requests = cache_keys.shape[0]
    block_len = cache_keys.shape[1]
    own_rows = tokens.shape[0]
    steps_count = tokens.shape[1]
    block_rows = head_gather(tokens).reshape((-1,) + tokens.shape[1:])
    triple = (
        jnp.einsum("rtd,kdc->rtkc", block_rows, w_qkv, preferred_element_type=jnp.float32)
        + qkv_bias
    )
    triple = triple.astype(jnp.bfloat16).reshape(
        block_rows.shape[0], block_rows.shape[1], 3 * local_width
    )
    gathered = jnp.concatenate([triple, block_rows], axis=2)
    head_shape = (requests, steps_count, local_heads, HDIM)
    queries = gathered[:, :, :local_width].reshape(head_shape)
    new_keys = gathered[:, :, local_width : 2 * local_width].reshape(head_shape)
    new_values = gathered[:, :, 2 * local_width : 3 * local_width].reshape(head_shape)
    fresh_keys = (
        jnp.einsum("rjd,dc->rjc", held_states, w_qkv[1], preferred_element_type=jnp.float32)
        + qkv_bias[1]
    ).astype(jnp.bfloat16)
    offset_pos = lax.axis_index("seq") * block_len
    positions = jnp.arange(block_len, dtype=jnp.int32)
    matches = (recompute_pos - offset_pos)[:, :, None] == positions[None, None, :]
    placed = jnp.einsum(
        "rjp,rjc->rpc", matches.astype(jnp.bfloat16), fresh_keys, preferred_element_type=jnp.float32
    ).astype(jnp.bfloat16)
    replaced = jnp.any(matches, axis=1)
    keys_here = jnp.where(replaced[:, :, None], placed, cache_keys)
    visible = ((offset_pos + positions)[None, :] < cache_len[:, None]) & (new_prompt[:, None] == 0)
    lane_head = jnp.arange(local_width, dtype=jnp.int32) // HDIM
    flat_queries = gathered[:, :, :local_width]
    zero = jnp.zeros((), flat_queries.dtype)
    scores = jnp.stack(
        [
            jnp.einsum(
                "rtc,rpc->rtp",
                jnp.where(lane_head == h, flat_queries, zero),
                keys_here,
                preferred_element_type=jnp.float32,
            )
            for h in range(local_heads)
        ],
        axis=2,
    ) * HDIM ** (-0.5)
    seen = visible[:, None, None, :]
    block_max = jnp.max(jnp.where(seen, scores, NEG), axis=-1)
    weights = jnp.exp(jnp.where(seen, scores - block_max[..., None], NEG)).astype(jnp.bfloat16)
    block_sum = jnp.sum(weights.astype(jnp.float32), axis=-1)
    block_out = jnp.zeros((requests, steps_count, local_width), jnp.float32)
    for h in range(local_heads):
        blended = jnp.einsum(
            "rtp,rpc->rtc", weights[:, :, h], cache_values, preferred_element_type=jnp.float32
        )
        block_out = jnp.where(lane_head == h, blended, block_out)
    order_t = jnp.arange(steps_count, dtype=jnp.int32)
    causal = (order_t[:, None] >= order_t[None, :])[None, :, None, :]
    new_max, new_sum, new_out = partial_attention(queries, new_keys, new_values, causal)
    rows = requests * steps_count
    flat = lambda m, s, o: (m.reshape(rows, local_heads), s.reshape(rows, local_heads), o.reshape(rows, local_width))
    cache_part = flat(block_max, block_sum, block_out)
    new_part = flat(new_max, new_sum, new_out)
    first = lax.axis_index("seq") == 0
    stats = pick(first, merge_rows(cache_part, new_part, HDIM), cache_part)
    attended = seq_attend(stats, HDIM).reshape(requests, steps_count, local_width)
    n_seq = lax.axis_size("seq")
    core = lax.axis_index("seq") % 2
    pair = [(i, i ^ 1) for i in range(n_seq)]
    ffw_half = w_up.shape[1] // 2
    bias_half = lax.dynamic_slice_in_dim(up_bias, core * ffw_half, ffw_half, 0)
    bias_hi = lax.reduce_precision(bias_half, exponent_bits=8, mantissa_bits=7)
    rest = bias_half - bias_hi
    bias_mid = lax.reduce_precision(rest, exponent_bits=8, mantissa_bits=7)
    bias_lo = rest - bias_mid
    pieces = jnp.stack([bias_hi, bias_mid, bias_lo]).astype(jnp.bfloat16)
    pieces = jnp.pad(pieces, ((0, 5), (0, 0)))
    up_rows = w_up.shape[0]
    w_up_all = lax.all_gather(
        jnp.concatenate(
            [lax.dynamic_slice_in_dim(w_up, core * ffw_half, ffw_half, 1), pieces], axis=0
        ),
        "head",
        axis=0,
    )
    got = w_up_all[:, up_rows : up_rows + 3].astype(jnp.float32)
    up_bias_all = got[:, 0] + got[:, 1] + got[:, 2]
    w_up_all = w_up_all[:, :up_rows]
    w_down_all = lax.all_gather(
        jnp.concatenate([lax.dynamic_slice_in_dim(w_down, core * ffw_half, ffw_half, 0), w_out]),
        "head",
        axis=0,
    )
    w_out_all = w_down_all[:, ffw_half:].reshape(-1, w_out.shape[1])
    w_down_all = w_down_all[:, :ffw_half]
    own_attended = lax.all_to_all(attended, "head", 0, 2, tiled=True)
    projected = jnp.einsum(
        "rtc,cd->rtd", own_attended, w_out_all, preferred_element_type=jnp.float32
    )
    normed = layer_norm(
        tokens.astype(jnp.float32) + projected + out_bias, attn_gain, attn_shift
    ).astype(jnp.bfloat16)
    hidden = jax.nn.gelu(
        jnp.einsum("rtd,hdf->rthf", normed, w_up_all, preferred_element_type=jnp.float32)
        + up_bias_all,
        approximate=False,
    ).astype(jnp.bfloat16)
    lowered = jnp.einsum("rthf,hfd->rtd", hidden, w_down_all, preferred_element_type=jnp.float32)
    lowered = lowered + lax.ppermute(lowered, "seq", pair)
    return layer_norm(normed.astype(jnp.float32) + lowered + down_bias, ffn_gain, ffn_shift).astype(
        jnp.bfloat16
    )


def solution(mesh):
    placed = (
        P("head", None, None),
        P(None, "seq", "head"),
        P(None, "seq", "head"),
        P(None, "seq", None),
        P(None, "seq"),
        P(),
        P(),
        P(None, None, "head"),
        P(None, "head"),
        P("head", None),
        P(),
        P(),
        P(),
        P(None, "head"),
        P("head"),
        P("head", None),
        P(),
        P(),
        P(),
    )
    return jax.shard_map(
        on_device, mesh=mesh, in_specs=placed, out_specs=P("head", None, None), check_vma=False
    )
```

```python
import jax
import jax.numpy as jnp
from jax import lax
from jax.sharding import PartitionSpec as P

HDIM = 64


NEG = -1e30
EPS = 1e-05


def layer_norm(values, norm_gain, norm_bias):
    center = jnp.mean(values, axis=-1, keepdims=True)
    spread = values - center
    second = jnp.mean(spread * spread, axis=-1, keepdims=True)
    return spread * lax.rsqrt(second + EPS) * norm_gain + norm_bias


def merge_pair(first_part, second_part):
    first_max, first_sum, first_out = first_part
    second_max, second_sum, second_out = second_part
    joint_max = jnp.maximum(first_max, second_max)
    first_scale = jnp.exp(first_max - joint_max)
    second_scale = jnp.exp(second_max - joint_max)
    return (
        joint_max,
        first_sum * first_scale + second_sum * second_scale,
        first_out * first_scale[..., None] + second_out * second_scale[..., None],
    )


def partial_attention(queries, keys_here, values_here, visible):
    scores = jnp.einsum(
        "rthe,rphe->rthp", queries, keys_here, preferred_element_type=jnp.float32
    ) * HDIM ** (-0.5)
    highest = jnp.max(jnp.where(visible, scores, NEG), axis=-1)
    weights = jnp.exp(jnp.where(visible, scores - highest[..., None], NEG)).astype(jnp.bfloat16)
    totals = jnp.sum(weights.astype(jnp.float32), axis=-1)
    blended = jnp.einsum(
        "rthp,rphe->rthe", weights, values_here, preferred_element_type=jnp.float32
    )
    return (highest, totals, blended)


def merge_rows(mine, theirs, width):
    top, total, out = mine
    o_top, o_total, o_out = theirs
    joint = jnp.maximum(top, o_top)
    scale = jnp.exp(top - joint)
    o_scale = jnp.exp(o_top - joint)
    out = out * jnp.repeat(scale, width, axis=1) + o_out * jnp.repeat(o_scale, width, axis=1)
    return (joint, total * scale + o_total * o_scale, out)


def exchange(stats, pairs):
    top, total, out = stats
    rows, heads = top.shape
    lanes = out.shape[1]
    flat = jnp.concatenate([top, total], axis=1).reshape(-1)
    fill = (-flat.size) % lanes
    flat = jnp.pad(flat, (0, fill)).reshape(-1, lanes)
    other = lax.ppermute(jnp.concatenate([out, flat], axis=0), "seq", pairs)
    o_out = other[:rows]
    o_flat = other[rows:].reshape(-1)[: rows * 2 * heads].reshape(rows, 2 * heads)
    return (o_flat[:, :heads], o_flat[:, heads:], o_out)


def pick(flag, when_set, when_clear):
    return jax.tree.map(lambda a, b: jnp.where(flag, a, b), when_set, when_clear)


def seq_attend(stats, width):
    n_seq = lax.axis_size("seq")
    me = lax.axis_index("seq")
    rows = stats[2].shape[0]
    bit = 1
    scatter_bits = []
    while bit < n_seq and rows % 16 == 0 and len(scatter_bits) < 2:
        half = rows // 2
        upper = (me // bit) % 2 == 1
        low = jax.tree.map(lambda a: a[:half], stats)
        high = jax.tree.map(lambda a: a[half:], stats)
        keep = pick(upper, high, low)
        send = pick(upper, low, high)
        other = exchange(send, [(i, i ^ bit) for i in range(n_seq)])
        stats = merge_rows(keep, other, width)
        scatter_bits.append(bit)
        rows = half
        bit *= 2
    while bit < n_seq:
        if bit * 4 == n_seq:
            group = [stats]
            for k in (1, 2, 3):
                group.append(exchange(stats, [(i, i ^ (k * bit)) for i in range(n_seq)]))
            stacked = jax.tree.map(lambda *a: jnp.stack(a), *group)
            mine = (me // bit) % 4
            block = lambda j: jax.tree.map(lambda a: a[mine ^ j], stacked)
            low = merge_rows(block(0), block(1), width)
            high = merge_rows(block(2), block(3), width)
            stats = merge_rows(low, high, width)
            break
        other = exchange(stats, [(i, i ^ bit) for i in range(n_seq)])
        stats = merge_rows(stats, other, width)
        bit *= 2
    top, total, out = stats
    attended = (out / jnp.repeat(total, width, axis=1)).astype(jnp.bfloat16)
    for bit in reversed(scatter_bits):
        upper = (me // bit) % 2 == 1
        other = lax.ppermute(attended, "seq", [(i, i ^ bit) for i in range(n_seq)])
        attended = jnp.where(
            upper,
            jnp.concatenate([other, attended], axis=0),
            jnp.concatenate([attended, other], axis=0),
        )
    return attended


def head_gather(x):
    n_head = lax.axis_size("head")
    me = lax.axis_index("head")
    parts = [x]
    for shift in range(1, n_head):
        parts.append(lax.ppermute(x, "head", [(i, (i + shift) % n_head) for i in range(n_head)]))
    stacked = jnp.stack(parts)
    order = (me - jnp.arange(n_head)) % n_head
    return jnp.take(stacked, order, axis=0)

def on_device(
    tokens,
    cache_keys,
    cache_values,
    held_states,
    recompute_pos,
    cache_len,
    new_prompt,
    w_qkv,
    qkv_bias,
    w_out,
    out_bias,
    attn_gain,
    attn_shift,
    w_up,
    up_bias,
    w_down,
    down_bias,
    ffn_gain,
    ffn_shift,
):
    local_width = w_qkv.shape[2]
    local_heads = local_width // HDIM
    requests = cache_keys.shape[0]
    block_len = cache_keys.shape[1]
    own_rows = tokens.shape[0]
    steps_count = tokens.shape[1]
    block_rows = head_gather(tokens).reshape((-1,) + tokens.shape[1:])
    triple = (
        jnp.einsum("rtd,kdc->rtkc", block_rows, w_qkv, preferred_element_type=jnp.float32)
        + qkv_bias
    )
    triple = triple.astype(jnp.bfloat16).reshape(
        block_rows.shape[0], block_rows.shape[1], 3 * local_width
    )
    gathered = jnp.concatenate([triple, block_rows], axis=2)
    head_shape = (requests, steps_count, local_heads, HDIM)
    queries = gathered[:, :, :local_width].reshape(head_shape)
    new_keys = gathered[:, :, local_width : 2 * local_width].reshape(head_shape)
    new_values = gathered[:, :, 2 * local_width : 3 * local_width].reshape(head_shape)
    fresh_keys = (
        jnp.einsum("rjd,dc->rjc", held_states, w_qkv[1], preferred_element_type=jnp.float32)
        + qkv_bias[1]
    ).astype(jnp.bfloat16)
    offset_pos = lax.axis_index("seq") * block_len
    positions = jnp.arange(block_len, dtype=jnp.int32)
    matches = (recompute_pos - offset_pos)[:, :, None] == positions[None, None, :]
    placed = jnp.einsum(
        "rjp,rjc->rpc", matches.astype(jnp.bfloat16), fresh_keys, preferred_element_type=jnp.float32
    ).astype(jnp.bfloat16)
    replaced = jnp.any(matches, axis=1)
    keys_here = jnp.where(replaced[:, :, None], placed, cache_keys)
    visible = ((offset_pos + positions)[None, :] < cache_len[:, None]) & (new_prompt[:, None] == 0)
    lane_head = jnp.arange(local_width, dtype=jnp.int32) // HDIM
    flat_queries = gathered[:, :, :local_width]
    zero = jnp.zeros((), flat_queries.dtype)
    scores = jnp.stack(
        [
            jnp.einsum(
                "rtc,rpc->rtp",
                jnp.where(lane_head == h, flat_queries, zero),
                keys_here,
                preferred_element_type=jnp.float32,
            )
            for h in range(local_heads)
        ],
        axis=2,
    ) * HDIM ** (-0.5)
    seen = visible[:, None, None, :]
    block_max = jnp.max(jnp.where(seen, scores, NEG), axis=-1)
    weights = jnp.exp(jnp.where(seen, scores - block_max[..., None], NEG)).astype(jnp.bfloat16)
    block_sum = jnp.sum(weights.astype(jnp.float32), axis=-1)
    block_out = jnp.zeros((requests, steps_count, local_width), jnp.float32)
    for h in range(local_heads):
        blended = jnp.einsum(
            "rtp,rpc->rtc", weights[:, :, h], cache_values, preferred_element_type=jnp.float32
        )
        block_out = jnp.where(lane_head == h, blended, block_out)
    order_t = jnp.arange(steps_count, dtype=jnp.int32)
    causal = (order_t[:, None] >= order_t[None, :])[None, :, None, :]
    flat_new_keys = gathered[:, :, local_width : 2 * local_width]
    flat_new_values = gathered[:, :, 2 * local_width : 3 * local_width]
    new_scores = jnp.stack(
        [
            jnp.einsum(
                "rtc,ruc->rtu",
                jnp.where(lane_head == h, flat_queries, zero),
                flat_new_keys,
                preferred_element_type=jnp.float32,
            )
            for h in range(local_heads)
        ],
        axis=2,
    ) * HDIM ** (-0.5)
    new_max = jnp.max(jnp.where(causal, new_scores, NEG), axis=-1)
    new_weights = jnp.exp(jnp.where(causal, new_scores - new_max[..., None], NEG)).astype(
        jnp.bfloat16
    )
    new_sum = jnp.sum(new_weights.astype(jnp.float32), axis=-1)
    new_out = jnp.zeros((requests, steps_count, local_width), jnp.float32)
    for h in range(local_heads):
        blended = jnp.einsum(
            "rtu,ruc->rtc", new_weights[:, :, h], flat_new_values, preferred_element_type=jnp.float32
        )
        new_out = jnp.where(lane_head == h, blended, new_out)
    rows = requests * steps_count
    flat = lambda m, s, o: (m.reshape(rows, local_heads), s.reshape(rows, local_heads), o.reshape(rows, local_width))
    cache_part = flat(block_max, block_sum, block_out)
    new_part = flat(new_max, new_sum, new_out)
    first = lax.axis_index("seq") == 0
    stats = pick(first, merge_rows(cache_part, new_part, HDIM), cache_part)
    attended = seq_attend(stats, HDIM).reshape(requests, steps_count, local_width)
    n_seq = lax.axis_size("seq")
    core = lax.axis_index("seq") % 2
    pair = [(i, i ^ 1) for i in range(n_seq)]
    ffw_half = w_up.shape[1] // 2
    bias_half = lax.dynamic_slice_in_dim(up_bias, core * ffw_half, ffw_half, 0)
    bias_hi = lax.reduce_precision(bias_half, exponent_bits=8, mantissa_bits=7)
    rest = bias_half - bias_hi
    bias_mid = lax.reduce_precision(rest, exponent_bits=8, mantissa_bits=7)
    bias_lo = rest - bias_mid
    pieces = jnp.stack([bias_hi, bias_mid, bias_lo]).astype(jnp.bfloat16)
    pieces = jnp.pad(pieces, ((0, 5), (0, 0)))
    up_rows = w_up.shape[0]
    w_up_all = lax.all_gather(
        jnp.concatenate(
            [lax.dynamic_slice_in_dim(w_up, core * ffw_half, ffw_half, 1), pieces], axis=0
        ),
        "head",
        axis=0,
    )
    got = w_up_all[:, up_rows : up_rows + 3].astype(jnp.float32)
    up_bias_all = got[:, 0] + got[:, 1] + got[:, 2]
    w_up_all = w_up_all[:, :up_rows]
    w_down_all = lax.all_gather(
        jnp.concatenate([lax.dynamic_slice_in_dim(w_down, core * ffw_half, ffw_half, 0), w_out]),
        "head",
        axis=0,
    )
    w_out_all = w_down_all[:, ffw_half:].reshape(-1, w_out.shape[1])
    w_down_all = w_down_all[:, :ffw_half]
    own_attended = lax.all_to_all(attended, "head", 0, 2, tiled=True)
    projected = jnp.einsum(
        "rtc,cd->rtd", own_attended, w_out_all, preferred_element_type=jnp.float32
    )
    normed = layer_norm(
        tokens.astype(jnp.float32) + projected + out_bias, attn_gain, attn_shift
    ).astype(jnp.bfloat16)
    hidden = jax.nn.gelu(
        jnp.einsum("rtd,hdf->rthf", normed, w_up_all, preferred_element_type=jnp.float32)
        + up_bias_all,
        approximate=False,
    ).astype(jnp.bfloat16)
    lowered = jnp.einsum("rthf,hfd->rtd", hidden, w_down_all, preferred_element_type=jnp.float32)
    lowered = lowered + lax.ppermute(lowered, "seq", pair)
    return layer_norm(normed.astype(jnp.float32) + lowered + down_bias, ffn_gain, ffn_shift).astype(
        jnp.bfloat16
    )


def solution(mesh):
    placed = (
        P("head", None, None),
        P(None, "seq", "head"),
        P(None, "seq", "head"),
        P(None, "seq", None),
        P(None, "seq"),
        P(),
        P(),
        P(None, None, "head"),
        P(None, "head"),
        P("head", None),
        P(),
        P(),
        P(),
        P(None, "head"),
        P("head"),
        P("head", None),
        P(),
        P(),
        P(),
    )
    return jax.shard_map(
        on_device, mesh=mesh, in_specs=placed, out_specs=P("head", None, None), check_vma=False
    )
```

```python
import jax
import jax.numpy as jnp
from jax import lax
from jax.sharding import PartitionSpec as P

HDIM = 64


NEG = -1e30
EPS = 1e-05


def layer_norm(values, norm_gain, norm_bias):
    center = jnp.mean(values, axis=-1, keepdims=True)
    spread = values - center
    second = jnp.mean(spread * spread, axis=-1, keepdims=True)
    return spread * lax.rsqrt(second + EPS) * norm_gain + norm_bias


def merge_pair(first_part, second_part):
    first_max, first_sum, first_out = first_part
    second_max, second_sum, second_out = second_part
    joint_max = jnp.maximum(first_max, second_max)
    first_scale = jnp.exp(first_max - joint_max)
    second_scale = jnp.exp(second_max - joint_max)
    return (
        joint_max,
        first_sum * first_scale + second_sum * second_scale,
        first_out * first_scale[..., None] + second_out * second_scale[..., None],
    )


def partial_attention(queries, keys_here, values_here, visible):
    scores = jnp.einsum(
        "rthe,rphe->rthp", queries, keys_here, preferred_element_type=jnp.float32
    ) * HDIM ** (-0.5)
    highest = jnp.max(jnp.where(visible, scores, NEG), axis=-1)
    weights = jnp.exp(jnp.where(visible, scores - highest[..., None], NEG)).astype(jnp.bfloat16)
    totals = jnp.sum(weights.astype(jnp.float32), axis=-1)
    blended = jnp.einsum(
        "rthp,rphe->rthe", weights, values_here, preferred_element_type=jnp.float32
    )
    return (highest, totals, blended)


def merge_rows(mine, theirs, width):
    top, total, out = mine
    o_top, o_total, o_out = theirs
    joint = jnp.maximum(top, o_top)
    scale = jnp.exp(top - joint)
    o_scale = jnp.exp(o_top - joint)
    out = out * jnp.repeat(scale, width, axis=1) + o_out * jnp.repeat(o_scale, width, axis=1)
    return (joint, total * scale + o_total * o_scale, out)


def exchange(stats, pairs):
    top, total, out = stats
    rows, heads = top.shape
    lanes = out.shape[1]
    flat = jnp.concatenate([top, total], axis=1).reshape(-1)
    fill = (-flat.size) % lanes
    flat = jnp.pad(flat, (0, fill)).reshape(-1, lanes)
    other = lax.ppermute(jnp.concatenate([out, flat], axis=0), "seq", pairs)
    o_out = other[:rows]
    o_flat = other[rows:].reshape(-1)[: rows * 2 * heads].reshape(rows, 2 * heads)
    return (o_flat[:, :heads], o_flat[:, heads:], o_out)


def pick(flag, when_set, when_clear):
    return jax.tree.map(lambda a, b: jnp.where(flag, a, b), when_set, when_clear)


def seq_attend(stats, width):
    n_seq = lax.axis_size("seq")
    me = lax.axis_index("seq")
    rows = stats[2].shape[0]
    bit = 1
    scatter_bits = []
    while bit < n_seq and rows % 16 == 0 and len(scatter_bits) < 2:
        half = rows // 2
        upper = (me // bit) % 2 == 1
        low = jax.tree.map(lambda a: a[:half], stats)
        high = jax.tree.map(lambda a: a[half:], stats)
        keep = pick(upper, high, low)
        send = pick(upper, low, high)
        other = exchange(send, [(i, i ^ bit) for i in range(n_seq)])
        stats = merge_rows(keep, other, width)
        scatter_bits.append(bit)
        rows = half
        bit *= 2
    while bit < n_seq:
        if bit * 4 == n_seq:
            group = [stats]
            for k in (1, 2, 3):
                group.append(exchange(stats, [(i, i ^ (k * bit)) for i in range(n_seq)]))
            stacked = jax.tree.map(lambda *a: jnp.stack(a), *group)
            mine = (me // bit) % 4
            block = lambda j: jax.tree.map(lambda a: a[mine ^ j], stacked)
            low = merge_rows(block(0), block(1), width)
            high = merge_rows(block(2), block(3), width)
            stats = merge_rows(low, high, width)
            break
        other = exchange(stats, [(i, i ^ bit) for i in range(n_seq)])
        stats = merge_rows(stats, other, width)
        bit *= 2
    top, total, out = stats
    attended = (out / jnp.repeat(total, width, axis=1)).astype(jnp.bfloat16)
    for bit in reversed(scatter_bits):
        upper = (me // bit) % 2 == 1
        other = lax.ppermute(attended, "seq", [(i, i ^ bit) for i in range(n_seq)])
        attended = jnp.where(
            upper,
            jnp.concatenate([other, attended], axis=0),
            jnp.concatenate([attended, other], axis=0),
        )
    return attended


def head_gather(x):
    n_head = lax.axis_size("head")
    me = lax.axis_index("head")
    step_up = [(i, (i + 1) % n_head) for i in range(n_head)]
    if n_head == 4:
        right = lax.ppermute(x, "head", step_up)
        left = lax.ppermute(x, "head", [(i, (i + 3) % n_head) for i in range(n_head)])
        parts = [x, right, lax.ppermute(right, "head", step_up), left]
    else:
        parts = [x]
        for shift in range(1, n_head):
            parts.append(
                lax.ppermute(x, "head", [(i, (i + shift) % n_head) for i in range(n_head)])
            )
    stacked = jnp.stack(parts)
    order = (me - jnp.arange(n_head)) % n_head
    return jnp.take(stacked, order, axis=0)

def on_device(
    tokens,
    cache_keys,
    cache_values,
    held_states,
    recompute_pos,
    cache_len,
    new_prompt,
    w_qkv,
    qkv_bias,
    w_out,
    out_bias,
    attn_gain,
    attn_shift,
    w_up,
    up_bias,
    w_down,
    down_bias,
    ffn_gain,
    ffn_shift,
):
    local_width = w_qkv.shape[2]
    local_heads = local_width // HDIM
    requests = cache_keys.shape[0]
    block_len = cache_keys.shape[1]
    own_rows = tokens.shape[0]
    steps_count = tokens.shape[1]
    block_rows = head_gather(tokens).reshape((-1,) + tokens.shape[1:])
    triple = (
        jnp.einsum("rtd,kdc->rtkc", block_rows, w_qkv, preferred_element_type=jnp.float32)
        + qkv_bias
    )
    triple = triple.astype(jnp.bfloat16).reshape(
        block_rows.shape[0], block_rows.shape[1], 3 * local_width
    )
    gathered = jnp.concatenate([triple, block_rows], axis=2)
    head_shape = (requests, steps_count, local_heads, HDIM)
    queries = gathered[:, :, :local_width].reshape(head_shape)
    new_keys = gathered[:, :, local_width : 2 * local_width].reshape(head_shape)
    new_values = gathered[:, :, 2 * local_width : 3 * local_width].reshape(head_shape)
    fresh_keys = (
        jnp.einsum("rjd,dc->rjc", held_states, w_qkv[1], preferred_element_type=jnp.float32)
        + qkv_bias[1]
    ).astype(jnp.bfloat16)
    offset_pos = lax.axis_index("seq") * block_len
    positions = jnp.arange(block_len, dtype=jnp.int32)
    matches = (recompute_pos - offset_pos)[:, :, None] == positions[None, None, :]
    placed = jnp.einsum(
        "rjp,rjc->rpc", matches.astype(jnp.bfloat16), fresh_keys, preferred_element_type=jnp.float32
    ).astype(jnp.bfloat16)
    replaced = jnp.any(matches, axis=1)
    keys_here = jnp.where(replaced[:, :, None], placed, cache_keys)
    visible = ((offset_pos + positions)[None, :] < cache_len[:, None]) & (new_prompt[:, None] == 0)
    lane_head = jnp.arange(local_width, dtype=jnp.int32) // HDIM
    flat_queries = gathered[:, :, :local_width]
    zero = jnp.zeros((), flat_queries.dtype)
    scores = jnp.stack(
        [
            jnp.einsum(
                "rtc,rpc->rtp",
                jnp.where(lane_head == h, flat_queries, zero),
                keys_here,
                preferred_element_type=jnp.float32,
            )
            for h in range(local_heads)
        ],
        axis=2,
    ) * HDIM ** (-0.5)
    seen = visible[:, None, None, :]
    block_max = jnp.max(jnp.where(seen, scores, NEG), axis=-1)
    weights = jnp.exp(jnp.where(seen, scores - block_max[..., None], NEG)).astype(jnp.bfloat16)
    block_sum = jnp.sum(weights.astype(jnp.float32), axis=-1)
    block_out = jnp.zeros((requests, steps_count, local_width), jnp.float32)
    for h in range(local_heads):
        blended = jnp.einsum(
            "rtp,rpc->rtc", weights[:, :, h], cache_values, preferred_element_type=jnp.float32
        )
        block_out = jnp.where(lane_head == h, blended, block_out)
    order_t = jnp.arange(steps_count, dtype=jnp.int32)
    causal = (order_t[:, None] >= order_t[None, :])[None, :, None, :]
    new_max, new_sum, new_out = partial_attention(queries, new_keys, new_values, causal)
    rows = requests * steps_count
    flat = lambda m, s, o: (m.reshape(rows, local_heads), s.reshape(rows, local_heads), o.reshape(rows, local_width))
    cache_part = flat(block_max, block_sum, block_out)
    new_part = flat(new_max, new_sum, new_out)
    first = lax.axis_index("seq") == 0
    stats = pick(first, merge_rows(cache_part, new_part, HDIM), cache_part)
    attended = seq_attend(stats, HDIM).reshape(requests, steps_count, local_width)
    n_seq = lax.axis_size("seq")
    core = lax.axis_index("seq") % 2
    pair = [(i, i ^ 1) for i in range(n_seq)]
    ffw_half = w_up.shape[1] // 2
    bias_half = lax.dynamic_slice_in_dim(up_bias, core * ffw_half, ffw_half, 0)
    bias_hi = lax.reduce_precision(bias_half, exponent_bits=8, mantissa_bits=7)
    rest = bias_half - bias_hi
    bias_mid = lax.reduce_precision(rest, exponent_bits=8, mantissa_bits=7)
    bias_lo = rest - bias_mid
    pieces = jnp.stack([bias_hi, bias_mid, bias_lo]).astype(jnp.bfloat16)
    pieces = jnp.pad(pieces, ((0, 5), (0, 0)))
    up_rows = w_up.shape[0]
    w_up_all = lax.all_gather(
        jnp.concatenate(
            [lax.dynamic_slice_in_dim(w_up, core * ffw_half, ffw_half, 1), pieces], axis=0
        ),
        "head",
        axis=0,
    )
    got = w_up_all[:, up_rows : up_rows + 3].astype(jnp.float32)
    up_bias_all = got[:, 0] + got[:, 1] + got[:, 2]
    w_up_all = w_up_all[:, :up_rows]
    w_down_all = lax.all_gather(
        jnp.concatenate([lax.dynamic_slice_in_dim(w_down, core * ffw_half, ffw_half, 0), w_out]),
        "head",
        axis=0,
    )
    w_out_all = w_down_all[:, ffw_half:].reshape(-1, w_out.shape[1])
    w_down_all = w_down_all[:, :ffw_half]
    own_attended = lax.all_to_all(attended, "head", 0, 2, tiled=True)
    projected = jnp.einsum(
        "rtc,cd->rtd", own_attended, w_out_all, preferred_element_type=jnp.float32
    )
    normed = layer_norm(
        tokens.astype(jnp.float32) + projected + out_bias, attn_gain, attn_shift
    ).astype(jnp.bfloat16)
    hidden = jax.nn.gelu(
        jnp.einsum("rtd,hdf->rthf", normed, w_up_all, preferred_element_type=jnp.float32)
        + up_bias_all,
        approximate=False,
    ).astype(jnp.bfloat16)
    lowered = jnp.einsum("rthf,hfd->rtd", hidden, w_down_all, preferred_element_type=jnp.float32)
    lowered = lowered + lax.ppermute(lowered, "seq", pair)
    return layer_norm(normed.astype(jnp.float32) + lowered + down_bias, ffn_gain, ffn_shift).astype(
        jnp.bfloat16
    )


def solution(mesh):
    placed = (
        P("head", None, None),
        P(None, "seq", "head"),
        P(None, "seq", "head"),
        P(None, "seq", None),
        P(None, "seq"),
        P(),
        P(),
        P(None, None, "head"),
        P(None, "head"),
        P("head", None),
        P(),
        P(),
        P(),
        P(None, "head"),
        P("head"),
        P("head", None),
        P(),
        P(),
        P(),
    )
    return jax.shard_map(
        on_device, mesh=mesh, in_specs=placed, out_specs=P("head", None, None), check_vma=False
    )
```

```python
import jax
import jax.numpy as jnp
from jax import lax
from jax.sharding import PartitionSpec as P

HDIM = 64


NEG = -1e30
EPS = 1e-05


def layer_norm(values, norm_gain, norm_bias):
    center = jnp.mean(values, axis=-1, keepdims=True)
    spread = values - center
    second = jnp.mean(spread * spread, axis=-1, keepdims=True)
    return spread * lax.rsqrt(second + EPS) * norm_gain + norm_bias


def merge_pair(first_part, second_part):
    first_max, first_sum, first_out = first_part
    second_max, second_sum, second_out = second_part
    joint_max = jnp.maximum(first_max, second_max)
    first_scale = jnp.exp(first_max - joint_max)
    second_scale = jnp.exp(second_max - joint_max)
    return (
        joint_max,
        first_sum * first_scale + second_sum * second_scale,
        first_out * first_scale[..., None] + second_out * second_scale[..., None],
    )


def partial_attention(queries, keys_here, values_here, visible):
    scores = jnp.einsum(
        "rthe,rphe->rthp", queries, keys_here, preferred_element_type=jnp.float32
    ) * HDIM ** (-0.5)
    highest = jnp.max(jnp.where(visible, scores, NEG), axis=-1)
    weights = jnp.exp(jnp.where(visible, scores - highest[..., None], NEG)).astype(jnp.bfloat16)
    totals = jnp.sum(weights.astype(jnp.float32), axis=-1)
    blended = jnp.einsum(
        "rthp,rphe->rthe", weights, values_here, preferred_element_type=jnp.float32
    )
    return (highest, totals, blended)


def merge_rows(mine, theirs, width):
    top, total, out = mine
    o_top, o_total, o_out = theirs
    joint = jnp.maximum(top, o_top)
    scale = jnp.exp(top - joint)
    o_scale = jnp.exp(o_top - joint)
    out = out * jnp.repeat(scale, width, axis=1) + o_out * jnp.repeat(o_scale, width, axis=1)
    return (joint, total * scale + o_total * o_scale, out)


def exchange(stats, pairs):
    top, total, out = stats
    rows, heads = top.shape
    lanes = out.shape[1]
    other = lax.ppermute(jnp.concatenate([out, top, total], axis=1), "seq", pairs)
    return (other[:, lanes : lanes + heads], other[:, lanes + heads :], other[:, :lanes])


def pick(flag, when_set, when_clear):
    return jax.tree.map(lambda a, b: jnp.where(flag, a, b), when_set, when_clear)


def seq_attend(stats, width):
    n_seq = lax.axis_size("seq")
    me = lax.axis_index("seq")
    rows = stats[2].shape[0]
    bit = 1
    scatter_bits = []
    while bit < n_seq and rows % 16 == 0 and len(scatter_bits) < 2:
        half = rows // 2
        upper = (me // bit) % 2 == 1
        low = jax.tree.map(lambda a: a[:half], stats)
        high = jax.tree.map(lambda a: a[half:], stats)
        keep = pick(upper, high, low)
        send = pick(upper, low, high)
        other = exchange(send, [(i, i ^ bit) for i in range(n_seq)])
        stats = merge_rows(keep, other, width)
        scatter_bits.append(bit)
        rows = half
        bit *= 2
    while bit < n_seq:
        if bit * 4 == n_seq:
            group = [stats]
            for k in (1, 2, 3):
                group.append(exchange(stats, [(i, i ^ (k * bit)) for i in range(n_seq)]))
            stacked = jax.tree.map(lambda *a: jnp.stack(a), *group)
            mine = (me // bit) % 4
            block = lambda j: jax.tree.map(lambda a: a[mine ^ j], stacked)
            low = merge_rows(block(0), block(1), width)
            high = merge_rows(block(2), block(3), width)
            stats = merge_rows(low, high, width)
            break
        other = exchange(stats, [(i, i ^ bit) for i in range(n_seq)])
        stats = merge_rows(stats, other, width)
        bit *= 2
    top, total, out = stats
    attended = (out / jnp.repeat(total, width, axis=1)).astype(jnp.bfloat16)
    for bit in reversed(scatter_bits):
        upper = (me // bit) % 2 == 1
        other = lax.ppermute(attended, "seq", [(i, i ^ bit) for i in range(n_seq)])
        attended = jnp.where(
            upper,
            jnp.concatenate([other, attended], axis=0),
            jnp.concatenate([attended, other], axis=0),
        )
    return attended


def head_gather(x):
    n_head = lax.axis_size("head")
    me = lax.axis_index("head")
    parts = [x]
    for shift in range(1, n_head):
        parts.append(lax.ppermute(x, "head", [(i, (i + shift) % n_head) for i in range(n_head)]))
    stacked = jnp.stack(parts)
    order = (me - jnp.arange(n_head)) % n_head
    return jnp.take(stacked, order, axis=0)

def on_device(
    tokens,
    cache_keys,
    cache_values,
    held_states,
    recompute_pos,
    cache_len,
    new_prompt,
    w_qkv,
    qkv_bias,
    w_out,
    out_bias,
    attn_gain,
    attn_shift,
    w_up,
    up_bias,
    w_down,
    down_bias,
    ffn_gain,
    ffn_shift,
):
    local_width = w_qkv.shape[2]
    local_heads = local_width // HDIM
    requests = cache_keys.shape[0]
    block_len = cache_keys.shape[1]
    own_rows = tokens.shape[0]
    steps_count = tokens.shape[1]
    block_rows = head_gather(tokens).reshape((-1,) + tokens.shape[1:])
    triple = (
        jnp.einsum("rtd,kdc->rtkc", block_rows, w_qkv, preferred_element_type=jnp.float32)
        + qkv_bias
    )
    triple = triple.astype(jnp.bfloat16).reshape(
        block_rows.shape[0], block_rows.shape[1], 3 * local_width
    )
    gathered = jnp.concatenate([triple, block_rows], axis=2)
    head_shape = (requests, steps_count, local_heads, HDIM)
    queries = gathered[:, :, :local_width].reshape(head_shape)
    new_keys = gathered[:, :, local_width : 2 * local_width].reshape(head_shape)
    new_values = gathered[:, :, 2 * local_width : 3 * local_width].reshape(head_shape)
    fresh_keys = (
        jnp.einsum("rjd,dc->rjc", held_states, w_qkv[1], preferred_element_type=jnp.float32)
        + qkv_bias[1]
    ).astype(jnp.bfloat16)
    offset_pos = lax.axis_index("seq") * block_len
    positions = jnp.arange(block_len, dtype=jnp.int32)
    matches = (recompute_pos - offset_pos)[:, :, None] == positions[None, None, :]
    placed = jnp.einsum(
        "rjp,rjc->rpc", matches.astype(jnp.bfloat16), fresh_keys, preferred_element_type=jnp.float32
    ).astype(jnp.bfloat16)
    replaced = jnp.any(matches, axis=1)
    keys_here = jnp.where(replaced[:, :, None], placed, cache_keys)
    visible = ((offset_pos + positions)[None, :] < cache_len[:, None]) & (new_prompt[:, None] == 0)
    lane_head = jnp.arange(local_width, dtype=jnp.int32) // HDIM
    flat_queries = gathered[:, :, :local_width]
    zero = jnp.zeros((), flat_queries.dtype)
    scores = jnp.stack(
        [
            jnp.einsum(
                "rtc,rpc->rtp",
                jnp.where(lane_head == h, flat_queries, zero),
                keys_here,
                preferred_element_type=jnp.float32,
            )
            for h in range(local_heads)
        ],
        axis=2,
    ) * HDIM ** (-0.5)
    seen = visible[:, None, None, :]
    block_max = jnp.max(jnp.where(seen, scores, NEG), axis=-1)
    weights = jnp.exp(jnp.where(seen, scores - block_max[..., None], NEG)).astype(jnp.bfloat16)
    block_sum = jnp.sum(weights.astype(jnp.float32), axis=-1)
    block_out = jnp.zeros((requests, steps_count, local_width), jnp.float32)
    for h in range(local_heads):
        blended = jnp.einsum(
            "rtp,rpc->rtc", weights[:, :, h], cache_values, preferred_element_type=jnp.float32
        )
        block_out = jnp.where(lane_head == h, blended, block_out)
    order_t = jnp.arange(steps_count, dtype=jnp.int32)
    causal = (order_t[:, None] >= order_t[None, :])[None, :, None, :]
    new_max, new_sum, new_out = partial_attention(queries, new_keys, new_values, causal)
    rows = requests * steps_count
    flat = lambda m, s, o: (m.reshape(rows, local_heads), s.reshape(rows, local_heads), o.reshape(rows, local_width))
    cache_part = flat(block_max, block_sum, block_out)
    new_part = flat(new_max, new_sum, new_out)
    first = lax.axis_index("seq") == 0
    stats = pick(first, merge_rows(cache_part, new_part, HDIM), cache_part)
    attended = seq_attend(stats, HDIM).reshape(requests, steps_count, local_width)
    n_seq = lax.axis_size("seq")
    core = lax.axis_index("seq") % 2
    pair = [(i, i ^ 1) for i in range(n_seq)]
    ffw_half = w_up.shape[1] // 2
    bias_half = lax.dynamic_slice_in_dim(up_bias, core * ffw_half, ffw_half, 0)
    bias_hi = lax.reduce_precision(bias_half, exponent_bits=8, mantissa_bits=7)
    rest = bias_half - bias_hi
    bias_mid = lax.reduce_precision(rest, exponent_bits=8, mantissa_bits=7)
    bias_lo = rest - bias_mid
    pieces = jnp.stack([bias_hi, bias_mid, bias_lo]).astype(jnp.bfloat16)
    pieces = jnp.pad(pieces, ((0, 5), (0, 0)))
    up_rows = w_up.shape[0]
    w_up_all = lax.all_gather(
        jnp.concatenate(
            [lax.dynamic_slice_in_dim(w_up, core * ffw_half, ffw_half, 1), pieces], axis=0
        ),
        "head",
        axis=0,
    )
    got = w_up_all[:, up_rows : up_rows + 3].astype(jnp.float32)
    up_bias_all = got[:, 0] + got[:, 1] + got[:, 2]
    w_up_all = w_up_all[:, :up_rows]
    w_down_all = lax.all_gather(
        jnp.concatenate([lax.dynamic_slice_in_dim(w_down, core * ffw_half, ffw_half, 0), w_out]),
        "head",
        axis=0,
    )
    w_out_all = w_down_all[:, ffw_half:].reshape(-1, w_out.shape[1])
    w_down_all = w_down_all[:, :ffw_half]
    own_attended = lax.all_to_all(attended, "head", 0, 2, tiled=True)
    projected = jnp.einsum(
        "rtc,cd->rtd", own_attended, w_out_all, preferred_element_type=jnp.float32
    )
    normed = layer_norm(
        tokens.astype(jnp.float32) + projected + out_bias, attn_gain, attn_shift
    ).astype(jnp.bfloat16)
    hidden = jax.nn.gelu(
        jnp.einsum("rtd,hdf->rthf", normed, w_up_all, preferred_element_type=jnp.float32)
        + up_bias_all,
        approximate=False,
    ).astype(jnp.bfloat16)
    lowered = jnp.einsum("rthf,hfd->rtd", hidden, w_down_all, preferred_element_type=jnp.float32)
    lowered = lowered + lax.ppermute(lowered, "seq", pair)
    return layer_norm(normed.astype(jnp.float32) + lowered + down_bias, ffn_gain, ffn_shift).astype(
        jnp.bfloat16
    )


def solution(mesh):
    placed = (
        P("head", None, None),
        P(None, "seq", "head"),
        P(None, "seq", "head"),
        P(None, "seq", None),
        P(None, "seq"),
        P(),
        P(),
        P(None, None, "head"),
        P(None, "head"),
        P("head", None),
        P(),
        P(),
        P(),
        P(None, "head"),
        P("head"),
        P("head", None),
        P(),
        P(),
        P(),
    )
    return jax.shard_map(
        on_device, mesh=mesh, in_specs=placed, out_specs=P("head", None, None), check_vma=False
    )
```
